128 devices in a mesh: sub: 8 (over x_hi, z), grp: 16 (over x_lo, y, core).
Axes of the slice: x: 4 (x_hi: 2, x_lo: 2; x = x_hi * 2 + x_lo), y: 4, z: 4, core: 2. Of those that a mesh axis runs over, the one named last changes fastest.
Arguments:
- potential_init: float32 [64, 128, 128, 128], P('grp', 'sub'), may hold values from -6 to 6
- conductivity: float32 [128, 128, 128], P('sub')
- inverse_rows: float32 [128, 24, 128, 128], P('sub', None, 'grp')
- electrodes: int32 [64, 2], replicated, may hold values from 0 to 2097151
- intersection_width: int32 [8], P('sub'), may hold values from 1 to 4, as said below
Outputs:
- potential: float32 [64, 128, 128, 128], P('grp', 'sub')
- residual_norms: float32 [64], P('grp')
The draws below stay inside these ranges and needn't reach their ends.
Inputs may be any that keep to these rules, and one draw needn't show every extreme that they name: `intersection_width`: some subdomain has intersection 4.
All inputs are finite; a program needn't handle non-finite values.
Results may differ from the reference program's by a relative error of at most 0.0003.
Values sent between devices are 32-bit elements; how exact they have to be, the bound alone decides.
No kernel may reach another device: no remote copies, remote signals or barrier semaphores. Data moves between devices by JAX's collectives and lax.ppermute only.
A program may use at most 448 MiB of HBM per device.

```python
import math
import jax
import jax.numpy as jnp
from jax import lax

SOURCES = 64
CX = 16
NZ = 128
WMAX = 4
ITERS = 2
NX = 128
NY = 128
N_SUB = 8


def rising_factor():
    x_pos = lax.broadcasted_iota(jnp.float32, (NX, NY, NZ), 0) / max(NX - 1, 1)
    y_pos = lax.broadcasted_iota(jnp.float32, (NX, NY, NZ), 1) / max(NY - 1, 1)
    return x_pos + y_pos


def draw_conductivity(key, part):
    rising = jnp.exp(math.log(3.0) * rising_factor())
    base = jnp.exp(jax.random.uniform(key, (NX, NY, NZ), jnp.float32, math.log(0.6), math.log(1.5)))
    return rising * base


def draw_inverse_rows(key, part):
    shape_all = (NX, CX + 2 * WMAX, NY, NZ)
    noise_key, diag_key = jax.random.split(key)
    x_ids = lax.broadcasted_iota(jnp.int32, shape_all, 0)
    col_ids = lax.broadcasted_iota(jnp.int32, shape_all, 1)
    on_diag = col_ids == x_ids % CX + WMAX
    x_pos = lax.broadcasted_iota(jnp.float32, shape_all, 0) / max(NX - 1, 1)
    y_pos = lax.broadcasted_iota(jnp.float32, shape_all, 2) / max(NY - 1, 1)
    scale_all = jnp.exp(-math.log(3.0) * (x_pos + y_pos)) / 7.0
    noise = 0.03 * jax.random.normal(noise_key, shape_all, jnp.float32)
    diagonal = 1.0 + 0.2 * jax.random.uniform(diag_key, shape_all, jnp.float32, -1.0, 1.0)
    return scale_all * (jnp.where(on_diag, diagonal, 0.0) + noise)


def draw_intersection_width(key, part):
    widths = jax.random.randint(key, (N_SUB,), 1, WMAX + 1, dtype=jnp.int32)
    chosen_slab = jax.random.randint(jax.random.fold_in(key, 7), (), 0, N_SUB, dtype=jnp.int32)
    return jnp.where(jnp.arange(N_SUB, dtype=jnp.int32) == chosen_slab, WMAX, widths).astype(jnp.int32)


def set_ends(entries, rng, low, largest):
    index_at = [jax.random.randint(jax.random.fold_in(rng, axis), (), 0, length) for axis, length in enumerate(entries.shape)]
    longest = entries.shape.index(max(entries.shape))
    next_to = index_at[:longest] + [(index_at[longest] + 1) % entries.shape[longest]] + index_at[longest + 1:]
    return entries.at[tuple(index_at)].set(low).at[tuple(next_to)].set(largest)


def level_of(own_key, dims, shards, smallest, high):
    loudness, own = 1.0, jax.random.fold_in(own_key, 6)
    for dim, parts in shards:
        heights = jnp.exp(jax.random.uniform(jax.random.fold_in(own, dim), (parts,), jnp.float32, smallest / len(shards), high / len(shards)))
        loudness = loudness * jnp.repeat(heights, dims[dim] // parts).reshape([-1 if axis == dim else 1 for axis in range(len(dims))])
    return loudness


def scatter_about(rng, shape, width, bound, shards=(), kind=jnp.bfloat16):
    entries = jax.random.normal(rng, shape, jnp.float32) * width
    if len(shards) > 0:
        entries = level_of(rng, shape, shards, -0.22, 0.18) * entries
    return jnp.clip(entries, min=-bound, max=bound).astype(kind)


def setup_inputs(seed: int = 0) -> dict:
    key_list = jax.random.split(jax.random.key(seed), 6)
    potential_init = scatter_about(key_list[0], (SOURCES, NX, NY, NZ), 1.0, 6.0, ((0, 16), (1, 8)), jnp.float32)
    conductivity = draw_conductivity(jax.random.fold_in(key_list[5], 71), 0)
    inverse_rows = draw_inverse_rows(jax.random.fold_in(key_list[5], 71), 0)
    electrodes = set_ends(jax.random.randint(key_list[3], (SOURCES, 2), 0, NX * NY * NZ), jax.random.fold_in(key_list[3], 1), 0, (NX * NY * NZ) - 1).astype(jnp.int32)
    intersection_width = draw_intersection_width(jax.random.fold_in(key_list[5], 71), 0)
    return {"potential_init": potential_init, "conductivity": conductivity, "inverse_rows": inverse_rows, "electrodes": electrodes, "intersection_width": intersection_width}


CURRENT = 16.0
MASS = 1.0

def neighbours(padded):
    return [padded[..., 2:, 1:-1, 1:-1], padded[..., :-2, 1:-1, 1:-1], padded[..., 1:-1, 2:, 1:-1], padded[..., 1:-1, :-2, 1:-1], padded[..., 1:-1, 1:-1, 2:], padded[..., 1:-1, 1:-1, :-2]]

def face_terms(conduct_pad):
    center_cells = conduct_pad[1:-1, 1:-1, 1:-1]
    face_coefs = [0.5 * (center_cells + beside_cell) for beside_cell in neighbours(conduct_pad)]
    center_coef = MASS * center_cells
    for face_coef in face_coefs:
        center_coef = center_coef + face_coef
    return (center_coef, face_coefs)

def apply_operator(values_in, padded, center_coef, face_coefs):
    image = center_coef * values_in
    for face_coef, beside_cell in zip(face_coefs, neighbours(padded)):
        image = image - face_coef * beside_cell
    return image

def reference(potential_init, conductivity, inverse_rows, electrodes, intersection_width):
    center_coef, face_coefs = face_terms(jnp.pad(conductivity, 1))
    x_ids = lax.broadcasted_iota(jnp.int32, (NX, NY, NZ), 0)
    y_ids = lax.broadcasted_iota(jnp.int32, (NX, NY, NZ), 1)
    z_ids = lax.broadcasted_iota(jnp.int32, (NX, NY, NZ), 2)
    flat_ids = (x_ids * NY + y_ids) * NZ + z_ids
    column_ids = jnp.arange(CX + 2 * WMAX, dtype=jnp.int32)

    def solve_source(pair):
        potential, electrode_pair = pair
        first = (flat_ids == electrode_pair[0]).astype(jnp.float32)
        second = (flat_ids == electrode_pair[1]).astype(jnp.float32)
        source_term = CURRENT * first - CURRENT * second
        for sweep in range(ITERS):
            residual = source_term - apply_operator(potential, jnp.pad(potential, 1), center_coef, face_coefs)
            widened = jnp.pad(residual, ((WMAX, WMAX), (0, 0), (0, 0)))
            pieces = []
            for slab in range(N_SUB):
                reach = intersection_width[slab]
                intersection_mask = ((column_ids >= WMAX - reach) & (column_ids < CX + WMAX + reach)).astype(jnp.float32)[:, None, None]
                extended_resid = widened[slab * CX:slab * CX + CX + 2 * WMAX] * intersection_mask
                pieces.append(jnp.einsum('ijyz,jyz->iyz', inverse_rows[slab * CX:(slab + 1) * CX], extended_resid, precision=lax.Precision.HIGHEST))
            potential = potential + jnp.concatenate(pieces, axis=0)
        residual = source_term - apply_operator(potential, jnp.pad(potential, 1), center_coef, face_coefs)
        norm_value = jnp.sqrt(jnp.sum(residual * residual) / float(NX * NY * NZ))
        return (potential, norm_value)
    potential, residual_norms = lax.map(solve_source, (potential_init, electrodes))
    return (potential, residual_norms)
```

```python
import jax
import jax.numpy as jnp
from jax import lax
from jax.sharding import Mesh, PartitionSpec as P

ITERS = 2


CURRENT = 16.0
MASS = 1.0

CHIP_AXES = ("xl", "y")
CORE = "core"
GRP = ("xl", "y", "core")


def extended_2(cells, sides, width):
    for axis, dim in sides:
        count = lax.axis_size(axis)
        ends = count - 1
        head = lax.slice_in_dim(cells, 0, width, axis=dim)
        tail = lax.slice_in_dim(cells, cells.shape[dim] - width, cells.shape[dim], axis=dim)
        cells = jnp.concatenate(
            [
                lax.ppermute(tail, axis, [(i, (i + 1) % count) for i in range(ends)]),
                cells,
                lax.ppermute(head, axis, [((i + 1) % count, i) for i in range(ends)]),
            ],
            axis=dim,
        )
    return cells


def neighbours(padded):
    return [
        padded[..., 2:, 1:-1, 1:-1],
        padded[..., :-2, 1:-1, 1:-1],
        padded[..., 1:-1, 2:, 1:-1],
        padded[..., 1:-1, :-2, 1:-1],
        padded[..., 1:-1, 1:-1, 2:],
        padded[..., 1:-1, 1:-1, :-2],
    ]


def face_terms(conduct_pad):
    center_cells = conduct_pad[1:-1, 1:-1, 1:-1]
    face_coefs = [0.5 * (center_cells + beside_cell) for beside_cell in neighbours(conduct_pad)]
    center_coef = MASS * center_cells
    for face_coef in face_coefs:
        center_coef = center_coef + face_coef
    return (center_coef, face_coefs)


def apply_operator(values_in, padded, center_coef, face_coefs):
    image = center_coef * values_in
    for face_coef, beside_cell in zip(face_coefs, neighbours(padded)):
        image = image - face_coef * beside_cell
    return image


def source_block(pairs, x_start, width_x, rows_y, full_y, depth):
    x_ids = x_start + lax.broadcasted_iota(jnp.int32, (width_x, rows_y, depth), 0)
    y_ids = lax.broadcasted_iota(jnp.int32, (width_x, rows_y, depth), 1)
    z_ids = lax.broadcasted_iota(jnp.int32, (width_x, rows_y, depth), 2)
    flat_ids = (x_ids * full_y + y_ids) * depth + z_ids
    first = (flat_ids[None] == pairs[:, 0][:, None, None, None]).astype(jnp.float32)
    second = (flat_ids[None] == pairs[:, 1][:, None, None, None]).astype(jnp.float32)
    return CURRENT * first - CURRENT * second


def on_device(potential_init, conductivity, inverse_rows, electrodes, intersection_width):
    local_src, width_x, full_y, depth = potential_init.shape
    n_core = lax.axis_size(CORE)
    core = lax.axis_index(CORE)
    grp_index = (lax.axis_index("xl") * lax.axis_size("y") + lax.axis_index("y")) * n_core + core
    sub_index = lax.axis_index("sub")
    extended = inverse_rows.shape[1]
    rows = inverse_rows.shape[2]
    blocks = full_y // (rows * n_core)
    margin = (extended - width_x) // 2
    cell_count = float(width_x * lax.axis_size("sub") * full_y * depth)
    column_ids = jnp.arange(extended, dtype=jnp.int32)
    reach = intersection_width[0]
    intersection_mask = (
        (column_ids >= margin - reach) & (column_ids < width_x + margin + reach)
    ).astype(jnp.float32)[:, None, None]
    inverse_mine = lax.all_gather(inverse_rows, CHIP_AXES, axis=2, tiled=True)
    conduct_rim = extended_2(conductivity, (("sub", 0),), 1)
    conduct_pad = jnp.pad(conduct_rim, ((0, 0), (1, 1), (1, 1)))
    x_start = sub_index * width_x
    center_coef, face_coefs = face_terms(conduct_pad)
    own_pairs = lax.dynamic_slice_in_dim(electrodes, grp_index * local_src, local_src, 0)
    source_term = source_block(own_pairs, x_start, width_x, full_y, full_y, depth)
    swap = [(0, 1), (1, 0)]

    def residual_of(potential):
        padded = extended_2(potential, (("sub", 1),), 1)
        padded = jnp.pad(padded, ((0, 0), (0, 0), (1, 1), (1, 1)))
        return source_term - apply_operator(potential, padded, center_coef, face_coefs)

    potential = potential_init
    for sweep in range(ITERS):
        residual = residual_of(potential)
        split = residual.reshape(local_src, width_x, blocks, n_core, rows, depth)
        own = lax.dynamic_index_in_dim(split, core, axis=3, keepdims=False)
        other = lax.dynamic_index_in_dim(split, 1 - core, axis=3, keepdims=False)
        got = lax.ppermute(other, CORE, swap)
        cells = jnp.concatenate([own, got], axis=0).reshape(2 * local_src, width_x, blocks * rows, depth)
        extended_resid = extended_2(cells, (("sub", 1),), margin) * intersection_mask
        correction = jnp.einsum(
            "ijyz,sjyz->siyz", inverse_mine, extended_resid, precision=lax.Precision.HIGHEST
        ).reshape(2 * local_src, width_x, blocks, rows, depth)
        mine = correction[:local_src]
        back = lax.ppermute(correction[local_src:], CORE, swap)
        first = jnp.where(core == 0, mine, back)
        second = jnp.where(core == 0, back, mine)
        update = jnp.stack([first, second], axis=3).reshape(potential.shape)
        potential = potential + update
    residual = residual_of(potential)
    totals = lax.psum(jnp.sum(residual * residual, axis=(1, 2, 3)), "sub")
    residual_norms = jnp.sqrt(totals / cell_count)
    return (potential, residual_norms)


def solution(mesh):
    n_sub, n_grp = mesh.devices.shape
    n_core = 2
    n_y = 4
    view = Mesh(
        mesh.devices.reshape(n_sub, n_grp // (n_y * n_core), n_y, n_core),
        ("sub", "xl", "y", "core"),
    )
    in_specs = (
        P(GRP, "sub", None, None),
        P("sub", None, None),
        P("sub", None, GRP, None),
        P(),
        P("sub"),
    )
    out_specs = (P(GRP, "sub", None, None), P(GRP))
    return jax.shard_map(
        on_device, mesh=view, in_specs=in_specs, out_specs=out_specs, check_vma=False
    )
```

```python
import jax
import jax.numpy as jnp
from jax import lax
from jax.sharding import Mesh, PartitionSpec as P
from jax.experimental import pallas as pl

def correction_kernel(inv_ref, ext_ref, out_ref):
    n_out, n_col = inv_ref.shape[0], inv_ref.shape[1]
    n_src = ext_ref.shape[0]

    def row(i, carry):
        accs = [None] * n_src
        for j in range(n_col):
            w = inv_ref[i, j]
            for s in range(n_src):
                term = w * ext_ref[s, j]
                accs[s] = term if accs[s] is None else accs[s] + term
        for s in range(n_src):
            out_ref[s, i] = accs[s]
        return carry

    lax.fori_loop(0, n_out, row, 0)

def correction_of(inv, ext, rows=8):
    n_out, n_col, ny, nz = inv.shape
    n_src = ext.shape[0]
    return pl.pallas_call(
        correction_kernel,
        grid=(ny // rows,),
        in_specs=[pl.BlockSpec((n_out, n_col, rows, nz), lambda b: (0, 0, b, 0)),
                  pl.BlockSpec((n_src, n_col, rows, nz), lambda b: (0, 0, b, 0))],
        out_specs=pl.BlockSpec((n_src, n_out, rows, nz), lambda b: (0, 0, b, 0)),
        out_shape=jax.ShapeDtypeStruct((n_src, n_out, ny, nz), jnp.float32),
    )(inv, ext)


ITERS = 2


CURRENT = 16.0
MASS = 1.0

CHIP_AXES = ("xl", "y")
CORE = "core"
GRP = ("xl", "y", "core")


def extended_2(cells, sides, width):
    for axis, dim in sides:
        count = lax.axis_size(axis)
        ends = count - 1
        head = lax.slice_in_dim(cells, 0, width, axis=dim)
        tail = lax.slice_in_dim(cells, cells.shape[dim] - width, cells.shape[dim], axis=dim)
        cells = jnp.concatenate(
            [
                lax.ppermute(tail, axis, [(i, (i + 1) % count) for i in range(ends)]),
                cells,
                lax.ppermute(head, axis, [((i + 1) % count, i) for i in range(ends)]),
            ],
            axis=dim,
        )
    return cells


def neighbours(padded):
    return [
        padded[..., 2:, 1:-1, 1:-1],
        padded[..., :-2, 1:-1, 1:-1],
        padded[..., 1:-1, 2:, 1:-1],
        padded[..., 1:-1, :-2, 1:-1],
        padded[..., 1:-1, 1:-1, 2:],
        padded[..., 1:-1, 1:-1, :-2],
    ]


def face_terms(conduct_pad):
    center_cells = conduct_pad[1:-1, 1:-1, 1:-1]
    face_coefs = [0.5 * (center_cells + beside_cell) for beside_cell in neighbours(conduct_pad)]
    center_coef = MASS * center_cells
    for face_coef in face_coefs:
        center_coef = center_coef + face_coef
    return (center_coef, face_coefs)


def apply_operator(values_in, padded, center_coef, face_coefs):
    image = center_coef * values_in
    for face_coef, beside_cell in zip(face_coefs, neighbours(padded)):
        image = image - face_coef * beside_cell
    return image


def source_block(pairs, x_start, width_x, rows_y, full_y, depth):
    x_ids = x_start + lax.broadcasted_iota(jnp.int32, (width_x, rows_y, depth), 0)
    y_ids = lax.broadcasted_iota(jnp.int32, (width_x, rows_y, depth), 1)
    z_ids = lax.broadcasted_iota(jnp.int32, (width_x, rows_y, depth), 2)
    flat_ids = (x_ids * full_y + y_ids) * depth + z_ids
    first = (flat_ids[None] == pairs[:, 0][:, None, None, None]).astype(jnp.float32)
    second = (flat_ids[None] == pairs[:, 1][:, None, None, None]).astype(jnp.float32)
    return CURRENT * first - CURRENT * second


def on_device(potential_init, conductivity, inverse_rows, electrodes, intersection_width):
    local_src, width_x, full_y, depth = potential_init.shape
    n_core = lax.axis_size(CORE)
    core = lax.axis_index(CORE)
    grp_index = (lax.axis_index("xl") * lax.axis_size("y") + lax.axis_index("y")) * n_core + core
    sub_index = lax.axis_index("sub")
    extended = inverse_rows.shape[1]
    rows = inverse_rows.shape[2]
    blocks = full_y // (rows * n_core)
    margin = (extended - width_x) // 2
    cell_count = float(width_x * lax.axis_size("sub") * full_y * depth)
    column_ids = jnp.arange(extended, dtype=jnp.int32)
    reach = intersection_width[0]
    intersection_mask = (
        (column_ids >= margin - reach) & (column_ids < width_x + margin + reach)
    ).astype(jnp.float32)[:, None, None]
    inverse_mine = lax.all_gather(inverse_rows, CHIP_AXES, axis=2, tiled=True)
    conduct_rim = extended_2(conductivity, (("sub", 0),), 1)
    conduct_pad = jnp.pad(conduct_rim, ((0, 0), (1, 1), (1, 1)))
    x_start = sub_index * width_x
    center_coef, face_coefs = face_terms(conduct_pad)
    own_pairs = lax.dynamic_slice_in_dim(electrodes, grp_index * local_src, local_src, 0)
    source_term = source_block(own_pairs, x_start, width_x, full_y, full_y, depth)
    swap = [(0, 1), (1, 0)]

    def residual_of(potential):
        padded = extended_2(potential, (("sub", 1),), 1)
        padded = jnp.pad(padded, ((0, 0), (0, 0), (1, 1), (1, 1)))
        return source_term - apply_operator(potential, padded, center_coef, face_coefs)

    potential = potential_init
    for sweep in range(ITERS):
        residual = residual_of(potential)
        split = residual.reshape(local_src, width_x, blocks, n_core, rows, depth)
        own = lax.dynamic_index_in_dim(split, core, axis=3, keepdims=False)
        other = lax.dynamic_index_in_dim(split, 1 - core, axis=3, keepdims=False)
        got = lax.ppermute(other, CORE, swap)
        cells = jnp.concatenate([own, got], axis=0).reshape(2 * local_src, width_x, blocks * rows, depth)
        extended_resid = extended_2(cells, (("sub", 1),), margin) * intersection_mask
        correction = correction_of(inverse_mine, extended_resid).reshape(
            2 * local_src, width_x, blocks, rows, depth
        )
        mine = correction[:local_src]
        back = lax.ppermute(correction[local_src:], CORE, swap)
        first = jnp.where(core == 0, mine, back)
        second = jnp.where(core == 0, back, mine)
        update = jnp.stack([first, second], axis=3).reshape(potential.shape)
        potential = potential + update
    residual = residual_of(potential)
    totals = lax.psum(jnp.sum(residual * residual, axis=(1, 2, 3)), "sub")
    residual_norms = jnp.sqrt(totals / cell_count)
    return (potential, residual_norms)


def solution(mesh):
    n_sub, n_grp = mesh.devices.shape
    n_core = 2
    n_y = 4
    view = Mesh(
        mesh.devices.reshape(n_sub, n_grp // (n_y * n_core), n_y, n_core),
        ("sub", "xl", "y", "core"),
    )
    in_specs = (
        P(GRP, "sub", None, None),
        P("sub", None, None),
        P("sub", None, GRP, None),
        P(),
        P("sub"),
    )
    out_specs = (P(GRP, "sub", None, None), P(GRP))
    return jax.shard_map(
        on_device, mesh=view, in_specs=in_specs, out_specs=out_specs, check_vma=False
    )
```

```python
import jax
import jax.numpy as jnp
from jax import lax
from jax.sharding import Mesh, PartitionSpec as P
from jax.experimental import pallas as pl
from jax.experimental.pallas import tpu as pltpu


def stencil_kernel(v_ref, lo_ref, hi_ref, st_ref, cc_ref, fxp_ref, fxm_ref, fyp_ref, fym_ref, fzp_ref, fzm_ref, out_ref):
    width = v_ref.shape[1]
    ny, nz = v_ref.shape[2], v_ref.shape[3]

    def plane(x, carry):
        v = v_ref[0, x]
        up = v_ref[0, jnp.minimum(x + 1, width - 1)]
        down = v_ref[0, jnp.maximum(x - 1, 0)]
        up = jnp.where(x == width - 1, hi_ref[0, 0], up)
        down = jnp.where(x == 0, lo_ref[0, 0], down)
        image = cc_ref[x] * v
        image = image - fxp_ref[x] * up
        image = image - fxm_ref[x] * down
        image = image - fyp_ref[x] * pltpu.roll(v, ny - 1, 0)
        image = image - fym_ref[x] * pltpu.roll(v, 1, 0)
        image = image - fzp_ref[x] * pltpu.roll(v, nz - 1, 1)
        image = image - fzm_ref[x] * pltpu.roll(v, 1, 1)
        out_ref[0, x] = st_ref[0, x] - image
        return carry

    lax.fori_loop(0, width, plane, 0)


def residual_kernel_call(v, lo, hi, st, coefs):
    n_src, width, ny, nz = v.shape
    src_block = pl.BlockSpec((1, width, ny, nz), lambda s: (s, 0, 0, 0))
    rim_block = pl.BlockSpec((1, 1, ny, nz), lambda s: (s, 0, 0, 0))
    coef_block = pl.BlockSpec((width, ny, nz), lambda s: (0, 0, 0))
    return pl.pallas_call(
        stencil_kernel,
        grid=(n_src,),
        in_specs=[src_block, rim_block, rim_block, src_block] + [coef_block] * 7,
        out_specs=src_block,
        out_shape=jax.ShapeDtypeStruct(v.shape, jnp.float32),
    )(v, lo, hi, st, *coefs)


def correction_kernel(inv_ref, ext_ref, out_ref):
    n_out, n_col = inv_ref.shape[0], inv_ref.shape[1]
    n_src = ext_ref.shape[0]

    def row(i, carry):
        accs = [None] * n_src
        for j in range(n_col):
            w = inv_ref[i, j]
            for s in range(n_src):
                term = w * ext_ref[s, j]
                accs[s] = term if accs[s] is None else accs[s] + term
        for s in range(n_src):
            out_ref[s, i] = accs[s]
        return carry

    lax.fori_loop(0, n_out, row, 0)

def correction_of(inv, ext, rows=8):
    n_out, n_col, ny, nz = inv.shape
    n_src = ext.shape[0]
    return pl.pallas_call(
        correction_kernel,
        grid=(ny // rows,),
        in_specs=[pl.BlockSpec((n_out, n_col, rows, nz), lambda b: (0, 0, b, 0)),
                  pl.BlockSpec((n_src, n_col, rows, nz), lambda b: (0, 0, b, 0))],
        out_specs=pl.BlockSpec((n_src, n_out, rows, nz), lambda b: (0, 0, b, 0)),
        out_shape=jax.ShapeDtypeStruct((n_src, n_out, ny, nz), jnp.float32),
    )(inv, ext)


ITERS = 2


CURRENT = 16.0
MASS = 1.0

CHIP_AXES = ("xl", "y")
CORE = "core"
GRP = ("xl", "y", "core")


def extended_2(cells, sides, width):
    for axis, dim in sides:
        count = lax.axis_size(axis)
        ends = count - 1
        head = lax.slice_in_dim(cells, 0, width, axis=dim)
        tail = lax.slice_in_dim(cells, cells.shape[dim] - width, cells.shape[dim], axis=dim)
        cells = jnp.concatenate(
            [
                lax.ppermute(tail, axis, [(i, (i + 1) % count) for i in range(ends)]),
                cells,
                lax.ppermute(head, axis, [((i + 1) % count, i) for i in range(ends)]),
            ],
            axis=dim,
        )
    return cells


def neighbours(padded):
    return [
        padded[..., 2:, 1:-1, 1:-1],
        padded[..., :-2, 1:-1, 1:-1],
        padded[..., 1:-1, 2:, 1:-1],
        padded[..., 1:-1, :-2, 1:-1],
        padded[..., 1:-1, 1:-1, 2:],
        padded[..., 1:-1, 1:-1, :-2],
    ]


def face_terms(conduct_pad):
    center_cells = conduct_pad[1:-1, 1:-1, 1:-1]
    face_coefs = [0.5 * (center_cells + beside_cell) for beside_cell in neighbours(conduct_pad)]
    center_coef = MASS * center_cells
    for face_coef in face_coefs:
        center_coef = center_coef + face_coef
    return (center_coef, face_coefs)


def apply_operator(values_in, padded, center_coef, face_coefs):
    image = center_coef * values_in
    for face_coef, beside_cell in zip(face_coefs, neighbours(padded)):
        image = image - face_coef * beside_cell
    return image


def source_block(pairs, x_start, width_x, rows_y, full_y, depth):
    x_ids = x_start + lax.broadcasted_iota(jnp.int32, (width_x, rows_y, depth), 0)
    y_ids = lax.broadcasted_iota(jnp.int32, (width_x, rows_y, depth), 1)
    z_ids = lax.broadcasted_iota(jnp.int32, (width_x, rows_y, depth), 2)
    flat_ids = (x_ids * full_y + y_ids) * depth + z_ids
    first = (flat_ids[None] == pairs[:, 0][:, None, None, None]).astype(jnp.float32)
    second = (flat_ids[None] == pairs[:, 1][:, None, None, None]).astype(jnp.float32)
    return CURRENT * first - CURRENT * second


def on_device(potential_init, conductivity, inverse_rows, electrodes, intersection_width):
    local_src, width_x, full_y, depth = potential_init.shape
    n_core = lax.axis_size(CORE)
    core = lax.axis_index(CORE)
    grp_index = (lax.axis_index("xl") * lax.axis_size("y") + lax.axis_index("y")) * n_core + core
    sub_index = lax.axis_index("sub")
    extended = inverse_rows.shape[1]
    rows = inverse_rows.shape[2]
    blocks = full_y // (rows * n_core)
    margin = (extended - width_x) // 2
    cell_count = float(width_x * lax.axis_size("sub") * full_y * depth)
    column_ids = jnp.arange(extended, dtype=jnp.int32)
    reach = intersection_width[0]
    intersection_mask = (
        (column_ids >= margin - reach) & (column_ids < width_x + margin + reach)
    ).astype(jnp.float32)[:, None, None]
    inverse_mine = lax.all_gather(inverse_rows, CHIP_AXES, axis=2, tiled=True)
    conduct_rim = extended_2(conductivity, (("sub", 0),), 1)
    conduct_pad = jnp.pad(conduct_rim, ((0, 0), (1, 1), (1, 1)))
    x_start = sub_index * width_x
    center_coef, face_coefs = face_terms(conduct_pad)
    own_pairs = lax.dynamic_slice_in_dim(electrodes, grp_index * local_src, local_src, 0)
    source_term = source_block(own_pairs, x_start, width_x, full_y, full_y, depth)
    swap = [(0, 1), (1, 0)]

    y_ids = lax.broadcasted_iota(jnp.int32, center_coef.shape, 1)
    z_ids = lax.broadcasted_iota(jnp.int32, center_coef.shape, 2)
    coefs = [
        center_coef,
        face_coefs[0],
        face_coefs[1],
        jnp.where(y_ids == full_y - 1, 0.0, face_coefs[2]),
        jnp.where(y_ids == 0, 0.0, face_coefs[3]),
        jnp.where(z_ids == depth - 1, 0.0, face_coefs[4]),
        jnp.where(z_ids == 0, 0.0, face_coefs[5]),
    ]
    n_sub = lax.axis_size("sub")

    def residual_of(potential):
        lo = lax.ppermute(potential[:, width_x - 1 :], "sub", [(i, i + 1) for i in range(n_sub - 1)])
        hi = lax.ppermute(potential[:, :1], "sub", [(i + 1, i) for i in range(n_sub - 1)])
        return residual_kernel_call(potential, lo, hi, source_term, coefs)

    potential = potential_init
    for sweep in range(ITERS):
        residual = residual_of(potential)
        split = residual.reshape(local_src, width_x, blocks, n_core, rows, depth)
        own = lax.dynamic_index_in_dim(split, core, axis=3, keepdims=False)
        other = lax.dynamic_index_in_dim(split, 1 - core, axis=3, keepdims=False)
        got = lax.ppermute(other, CORE, swap)
        cells = jnp.concatenate([own, got], axis=0).reshape(2 * local_src, width_x, blocks * rows, depth)
        extended_resid = extended_2(cells, (("sub", 1),), margin) * intersection_mask
        correction = correction_of(inverse_mine, extended_resid).reshape(
            2 * local_src, width_x, blocks, rows, depth
        )
        mine = correction[:local_src]
        back = lax.ppermute(correction[local_src:], CORE, swap)
        first = jnp.where(core == 0, mine, back)
        second = jnp.where(core == 0, back, mine)
        update = jnp.stack([first, second], axis=3).reshape(potential.shape)
        potential = potential + update
    residual = residual_of(potential)
    totals = lax.psum(jnp.sum(residual * residual, axis=(1, 2, 3)), "sub")
    residual_norms = jnp.sqrt(totals / cell_count)
    return (potential, residual_norms)


def solution(mesh):
    n_sub, n_grp = mesh.devices.shape
    n_core = 2
    n_y = 4
    view = Mesh(
        mesh.devices.reshape(n_sub, n_grp // (n_y * n_core), n_y, n_core),
        ("sub", "xl", "y", "core"),
    )
    in_specs = (
        P(GRP, "sub", None, None),
        P("sub", None, None),
        P("sub", None, GRP, None),
        P(),
        P("sub"),
    )
    out_specs = (P(GRP, "sub", None, None), P(GRP))
    return jax.shard_map(
        on_device, mesh=view, in_specs=in_specs, out_specs=out_specs, check_vma=False
    )
```

```python
import jax
import jax.numpy as jnp
from jax import lax
from jax.sharding import Mesh, PartitionSpec as P
from jax.experimental import pallas as pl
from jax.experimental.pallas import tpu as pltpu

ITERS = 2
INTERPRET = False

CURRENT = 16.0
MASS = 1.0

CHIP_AXES = ("xl", "y")
CORE = "core"
GRP = ("xl", "y", "core")


def make_stencil_kernel(planes, has_rim):
    def kernel(*refs):
        if has_rim:
            v_ref, lo_ref, hi_ref = refs[:3]
            rest = refs[3:]
        else:
            v_ref, lo_ref, hi_ref = refs[0], None, None
            rest = refs[1:]
        st_ref, cc_ref, fxp_ref, fxm_ref, fyp_ref, fym_ref, fzp_ref, fzm_ref, out_ref = rest
        width = v_ref.shape[1]
        ny, nz = v_ref.shape[2], v_ref.shape[3]

        def load(q):
            if q < 0:
                return lo_ref[0, lo_ref.shape[1] + q]
            if q >= width:
                return hi_ref[0, q - width]
            return v_ref[0, q]

        for o, p in enumerate(planes):
            v = load(p)
            image = cc_ref[o] * v
            image = image - fxp_ref[o] * load(p + 1)
            image = image - fxm_ref[o] * load(p - 1)
            image = image - fyp_ref[o] * pltpu.roll(v, ny - 1, 0)
            image = image - fym_ref[o] * pltpu.roll(v, 1, 0)
            image = image - fzp_ref[o] * pltpu.roll(v, nz - 1, 1)
            image = image - fzm_ref[o] * pltpu.roll(v, 1, 1)
            out_ref[0, o] = st_ref[0, o] - image

    return kernel


def stencil_call(planes, v, rims, st, coefs):
    n_src, width, ny, nz = v.shape
    n_out = len(planes)
    own_block = pl.BlockSpec((1, width, ny, nz), lambda s: (s, 0, 0, 0))
    out_block = pl.BlockSpec((1, n_out, ny, nz), lambda s: (s, 0, 0, 0))
    coef_block = pl.BlockSpec((n_out, ny, nz), lambda s: (0, 0, 0))
    rim_specs = [pl.BlockSpec((1, r.shape[1], ny, nz), lambda s: (s, 0, 0, 0)) for r in rims]
    return pl.pallas_call(
        make_stencil_kernel(tuple(planes), len(rims) > 0),
        grid=(n_src,),
        in_specs=[own_block] + rim_specs + [out_block] + [coef_block] * 7,
        out_specs=out_block,
        out_shape=jax.ShapeDtypeStruct((n_src, n_out, ny, nz), jnp.float32),
        interpret=INTERPRET,
    )(v, *rims, st, *coefs)


def make_correction_kernel(columns):
    def kernel(mask_ref, inv_ref, *refs):
        out_ref = refs[-1]
        pieces = refs[:-1]
        n_out = inv_ref.shape[0]
        halves = len(pieces) // 2

        def row(i, carry):
            accs = None
            for j, (piece, plane) in enumerate(columns):
                w = inv_ref[i, j] * mask_ref[j]
                terms = []
                for half in range(2):
                    src_ref = pieces[half * halves + piece]
                    for s in range(src_ref.shape[0]):
                        terms.append(w * src_ref[s, plane])
                accs = terms if accs is None else [a + t for a, t in zip(accs, terms)]
            for s, acc in enumerate(accs):
                out_ref[s, i] = acc
            return carry

        lax.fori_loop(0, n_out, row, 0)

    return kernel


def correction_call(mask, inv, own_pieces, got_pieces, columns, rows=8):
    n_out, n_col, ny, nz = inv.shape
    n_src = sum(p.shape[0] for p in own_pieces[:1]) * 2
    specs = [pl.BlockSpec((p.shape[0], p.shape[1], rows, nz), lambda b: (0, 0, b, 0)) for p in own_pieces + got_pieces]
    return pl.pallas_call(
        make_correction_kernel(tuple(columns)),
        grid=(ny // rows,),
        in_specs=[pl.BlockSpec(memory_space=pltpu.SMEM),
                  pl.BlockSpec((n_out, n_col, rows, nz), lambda b: (0, 0, b, 0))] + specs,
        out_specs=pl.BlockSpec((n_src, n_out, rows, nz), lambda b: (0, 0, b, 0)),
        out_shape=jax.ShapeDtypeStruct((n_src, n_out, ny, nz), jnp.float32),
        interpret=INTERPRET,
    )(mask, inv, *own_pieces, *got_pieces)


def rims_of(cells, depth_x, dim):
    count = lax.axis_size("sub")
    head = lax.slice_in_dim(cells, 0, depth_x, axis=dim)
    tail = lax.slice_in_dim(cells, cells.shape[dim] - depth_x, cells.shape[dim], axis=dim)
    lo = lax.ppermute(tail, "sub", [(i, i + 1) for i in range(count - 1)])
    hi = lax.ppermute(head, "sub", [(i + 1, i) for i in range(count - 1)])
    return lo, hi


def neighbours(padded):
    return [
        padded[..., 2:, 1:-1, 1:-1],
        padded[..., :-2, 1:-1, 1:-1],
        padded[..., 1:-1, 2:, 1:-1],
        padded[..., 1:-1, :-2, 1:-1],
        padded[..., 1:-1, 1:-1, 2:],
        padded[..., 1:-1, 1:-1, :-2],
    ]


def face_terms(conduct_pad):
    center_cells = conduct_pad[1:-1, 1:-1, 1:-1]
    face_coefs = [0.5 * (center_cells + beside_cell) for beside_cell in neighbours(conduct_pad)]
    center_coef = MASS * center_cells
    for face_coef in face_coefs:
        center_coef = center_coef + face_coef
    return (center_coef, face_coefs)


def source_block(pairs, x_start, width_x, rows_y, full_y, depth):
    x_ids = x_start + lax.broadcasted_iota(jnp.int32, (width_x, rows_y, depth), 0)
    y_ids = lax.broadcasted_iota(jnp.int32, (width_x, rows_y, depth), 1)
    z_ids = lax.broadcasted_iota(jnp.int32, (width_x, rows_y, depth), 2)
    flat_ids = (x_ids * full_y + y_ids) * depth + z_ids
    first = (flat_ids[None] == pairs[:, 0][:, None, None, None]).astype(jnp.float32)
    second = (flat_ids[None] == pairs[:, 1][:, None, None, None]).astype(jnp.float32)
    return CURRENT * first - CURRENT * second


def on_device(potential_init, conductivity, inverse_rows, electrodes, intersection_width):
    local_src, width_x, full_y, depth = potential_init.shape
    n_core = lax.axis_size(CORE)
    n_sub = lax.axis_size("sub")
    core = lax.axis_index(CORE)
    grp_index = (lax.axis_index("xl") * lax.axis_size("y") + lax.axis_index("y")) * n_core + core
    sub_index = lax.axis_index("sub")
    extended = inverse_rows.shape[1]
    rows = inverse_rows.shape[2]
    blocks = full_y // (rows * n_core)
    margin = (extended - width_x) // 2
    rim = margin + 1
    cell_count = float(width_x * n_sub * full_y * depth)
    x_start = sub_index * width_x
    column_ids = jnp.arange(extended, dtype=jnp.int32)
    reach = intersection_width[0]
    column_x = x_start - margin + column_ids
    column_mask = (
        (column_ids >= margin - reach)
        & (column_ids < width_x + margin + reach)
        & (column_x >= 0)
        & (column_x < width_x * n_sub)
    ).astype(jnp.float32)
    inverse_mine = lax.all_gather(inverse_rows, CHIP_AXES, axis=2, tiled=True)

    c_lo, c_hi = rims_of(conductivity, rim, 0)
    conduct_pad = jnp.pad(jnp.concatenate([c_lo, conductivity, c_hi], axis=0), ((0, 0), (1, 1), (1, 1)))
    center_coef, face_coefs = face_terms(conduct_pad)
    y_ids = lax.broadcasted_iota(jnp.int32, center_coef.shape, 1)
    z_ids = lax.broadcasted_iota(jnp.int32, center_coef.shape, 2)
    coefs = [
        center_coef,
        face_coefs[0],
        face_coefs[1],
        jnp.where(y_ids == full_y - 1, 0.0, face_coefs[2]),
        jnp.where(y_ids == 0, 0.0, face_coefs[3]),
        jnp.where(z_ids == depth - 1, 0.0, face_coefs[4]),
        jnp.where(z_ids == 0, 0.0, face_coefs[5]),
    ]
    own_pairs = lax.dynamic_slice_in_dim(electrodes, grp_index * local_src, local_src, 0)
    source_term = source_block(own_pairs, x_start - margin, extended, full_y, full_y, depth)

    mid_planes = list(range(1, width_x - 1))
    bnd_planes = list(range(-margin, 1)) + list(range(width_x - 1, width_x + margin))
    own_planes = list(range(width_x))

    def pick(arr, planes, axis):
        return jnp.concatenate([lax.slice_in_dim(arr, p + margin, p + margin + 1, axis=axis) for p in planes], axis=axis)

    def runs(planes):
        return [(p + margin) for p in planes]

    mid_coefs = [c[1 + margin : width_x - 1 + margin] for c in coefs]
    bnd_coefs = [jnp.concatenate([c[: margin + 1], c[width_x - 1 + margin :]], axis=0) for c in coefs]
    own_coefs = [c[margin : margin + width_x] for c in coefs]
    mid_st = source_term[:, 1 + margin : width_x - 1 + margin]
    bnd_st = jnp.concatenate([source_term[:, : margin + 1], source_term[:, width_x - 1 + margin :]], axis=1)
    own_st = source_term[:, margin : margin + width_x]

    columns = []
    for j in range(extended):
        p = j - margin
        if p in mid_planes:
            columns.append((0, mid_planes.index(p)))
        else:
            columns.append((1, bnd_planes.index(p)))

    swap = [(0, 1), (1, 0)]

    def swap_rows(piece):
        split = piece.reshape(local_src, piece.shape[1], blocks, n_core, rows, depth)
        own = lax.dynamic_index_in_dim(split, core, axis=3, keepdims=False).reshape(
            local_src, piece.shape[1], blocks * rows, depth)
        other = lax.dynamic_index_in_dim(split, 1 - core, axis=3, keepdims=False).reshape(
            local_src, piece.shape[1], blocks * rows, depth)
        return own, lax.ppermute(other, CORE, swap)

    potential = potential_init
    for sweep in range(ITERS):
        lo, hi = rims_of(potential, rim, 1)
        mid = stencil_call(mid_planes, potential, [], mid_st, mid_coefs)
        mid_own, mid_got = swap_rows(mid)
        bnd = stencil_call(bnd_planes, potential, [lo, hi], bnd_st, bnd_coefs)
        bnd_own, bnd_got = swap_rows(bnd)
        correction = correction_call(
            column_mask, inverse_mine, [mid_own, bnd_own], [mid_got, bnd_got], columns
        ).reshape(2 * local_src, width_x, blocks, rows, depth)
        mine = correction[:local_src]
        back = lax.ppermute(correction[local_src:], CORE, swap)
        first = jnp.where(core == 0, mine, back)
        second = jnp.where(core == 0, back, mine)
        update = jnp.stack([first, second], axis=3).reshape(potential.shape)
        potential = potential + update
    lo, hi = rims_of(potential, 1, 1)
    residual = stencil_call(own_planes, potential, [lo, hi], own_st, own_coefs)
    totals = lax.psum(jnp.sum(residual * residual, axis=(1, 2, 3)), "sub")
    residual_norms = jnp.sqrt(totals / cell_count)
    return (potential, residual_norms)


def solution(mesh):
    n_sub, n_grp = mesh.devices.shape
    n_core = 2
    n_y = 4
    view = Mesh(
        mesh.devices.reshape(n_sub, n_grp // (n_y * n_core), n_y, n_core),
        ("sub", "xl", "y", "core"),
    )
    in_specs = (
        P(GRP, "sub", None, None),
        P("sub", None, None),
        P("sub", None, GRP, None),
        P(),
        P("sub"),
    )
    out_specs = (P(GRP, "sub", None, None), P(GRP))
    return jax.shard_map(
        on_device, mesh=view, in_specs=in_specs, out_specs=out_specs, check_vma=False
    )
```

```python
import jax
import jax.numpy as jnp
from jax import lax
from jax.sharding import Mesh, PartitionSpec as P
from jax.experimental import pallas as pl
from jax.experimental.pallas import tpu as pltpu

ITERS = 2
INTERPRET = False

CURRENT = 16.0
MASS = 1.0

CHIP_AXES = ("xl", "y")
CORE = "core"
GRP = ("xl", "y", "core")


def make_stencil_kernel(planes, has_rim, mode):
    def kernel(core_ref, *refs):
        n_in = 3 if has_rim else 1
        v_ref = refs[0]
        lo_ref, hi_ref = (refs[1], refs[2]) if has_rim else (None, None)
        st_ref, cc_ref, fxp_ref, fxm_ref, fyp_ref, fym_ref, fzp_ref, fzm_ref = refs[n_in : n_in + 8]
        outs = refs[n_in + 8 :]
        width = v_ref.shape[1]
        ny, nz = v_ref.shape[2], v_ref.shape[3]
        core = core_ref[0]

        def load(q):
            if q < 0:
                return lo_ref[0, lo_ref.shape[1] + q]
            if q >= width:
                return hi_ref[0, q - width]
            return v_ref[0, q]

        total = None
        for o, p in enumerate(planes):
            v = load(p)
            image = cc_ref[o] * v
            image = image - fxp_ref[o] * load(p + 1)
            image = image - fxm_ref[o] * load(p - 1)
            image = image - fyp_ref[o] * pltpu.roll(v, ny - 1, 0)
            image = image - fym_ref[o] * pltpu.roll(v, 1, 0)
            image = image - fzp_ref[o] * pltpu.roll(v, nz - 1, 1)
            image = image - fzm_ref[o] * pltpu.roll(v, 1, 1)
            resid = st_ref[0, o] - image
            if mode == "norm":
                square = resid * resid
                total = square if total is None else total + square
                continue
            own_ref, other_ref = outs
            tile = 8
            for g in range(ny // (2 * tile)):
                first = resid[2 * g * tile : (2 * g + 1) * tile]
                second = resid[(2 * g + 1) * tile : (2 * g + 2) * tile]
                own_ref[0, o, g * tile : (g + 1) * tile] = jnp.where(core == 0, first, second)
                other_ref[0, o, g * tile : (g + 1) * tile] = jnp.where(core == 0, second, first)
        if mode == "norm":
            outs[0][0] = total.reshape(ny // 8, 8, nz).sum(axis=0)

    return kernel


def stencil_call(planes, core, v, rims, st, coefs, mode):
    n_src, width, ny, nz = v.shape
    n_out = len(planes)
    own_block = pl.BlockSpec((1, width, ny, nz), lambda s: (s, 0, 0, 0))
    st_block = pl.BlockSpec((1, n_out, ny, nz), lambda s: (s, 0, 0, 0))
    coef_block = pl.BlockSpec((n_out, ny, nz), lambda s: (0, 0, 0))
    rim_specs = [pl.BlockSpec((1, r.shape[1], ny, nz), lambda s: (s, 0, 0, 0)) for r in rims]
    if mode == "norm":
        out_specs = pl.BlockSpec((1, 8, nz), lambda s: (s, 0, 0))
        out_shape = jax.ShapeDtypeStruct((n_src, 8, nz), jnp.float32)
    else:
        half = pl.BlockSpec((1, n_out, ny // 2, nz), lambda s: (s, 0, 0, 0))
        out_specs = [half, half]
        out_shape = [jax.ShapeDtypeStruct((n_src, n_out, ny // 2, nz), jnp.float32)] * 2
    return pl.pallas_call(
        make_stencil_kernel(tuple(planes), len(rims) > 0, mode),
        grid=(n_src,),
        in_specs=[pl.BlockSpec(memory_space=pltpu.SMEM), own_block] + rim_specs + [st_block] + [coef_block] * 7,
        out_specs=out_specs,
        out_shape=out_shape,
        interpret=INTERPRET,
    )(core, v, *rims, st, *coefs)


def make_correction_kernel(columns):
    def kernel(mask_ref, inv_ref, *refs):
        out_ref = refs[-1]
        pieces = refs[:-1]
        n_out = inv_ref.shape[0]
        halves = len(pieces) // 2

        def row(i, carry):
            accs = None
            for j, (piece, plane) in enumerate(columns):
                w = inv_ref[i, j] * mask_ref[j]
                terms = []
                for half in range(2):
                    src_ref = pieces[half * halves + piece]
                    for s in range(src_ref.shape[0]):
                        terms.append(w * src_ref[s, plane])
                accs = terms if accs is None else [a + t for a, t in zip(accs, terms)]
            for s, acc in enumerate(accs):
                out_ref[s, i] = acc
            return carry

        lax.fori_loop(0, n_out, row, 0)

    return kernel


def correction_call(mask, inv, own_pieces, got_pieces, columns, rows=8):
    n_out, n_col, ny, nz = inv.shape
    n_src = sum(p.shape[0] for p in own_pieces[:1]) * 2
    specs = [pl.BlockSpec((p.shape[0], p.shape[1], rows, nz), lambda b: (0, 0, b, 0)) for p in own_pieces + got_pieces]
    return pl.pallas_call(
        make_correction_kernel(tuple(columns)),
        grid=(ny // rows,),
        in_specs=[pl.BlockSpec(memory_space=pltpu.SMEM),
                  pl.BlockSpec((n_out, n_col, rows, nz), lambda b: (0, 0, b, 0))] + specs,
        out_specs=pl.BlockSpec((n_src, n_out, rows, nz), lambda b: (0, 0, b, 0)),
        out_shape=jax.ShapeDtypeStruct((n_src, n_out, ny, nz), jnp.float32),
        interpret=INTERPRET,
    )(mask, inv, *own_pieces, *got_pieces)


def rims_of(cells, depth_x, dim):
    count = lax.axis_size("sub")
    head = lax.slice_in_dim(cells, 0, depth_x, axis=dim)
    tail = lax.slice_in_dim(cells, cells.shape[dim] - depth_x, cells.shape[dim], axis=dim)
    lo = lax.ppermute(tail, "sub", [(i, i + 1) for i in range(count - 1)])
    hi = lax.ppermute(head, "sub", [(i + 1, i) for i in range(count - 1)])
    return lo, hi


def neighbours(padded):
    return [
        padded[..., 2:, 1:-1, 1:-1],
        padded[..., :-2, 1:-1, 1:-1],
        padded[..., 1:-1, 2:, 1:-1],
        padded[..., 1:-1, :-2, 1:-1],
        padded[..., 1:-1, 1:-1, 2:],
        padded[..., 1:-1, 1:-1, :-2],
    ]


def face_terms(conduct_pad):
    center_cells = conduct_pad[1:-1, 1:-1, 1:-1]
    face_coefs = [0.5 * (center_cells + beside_cell) for beside_cell in neighbours(conduct_pad)]
    center_coef = MASS * center_cells
    for face_coef in face_coefs:
        center_coef = center_coef + face_coef
    return (center_coef, face_coefs)


def source_block(pairs, x_start, width_x, rows_y, full_y, depth):
    x_ids = x_start + lax.broadcasted_iota(jnp.int32, (width_x, rows_y, depth), 0)
    y_ids = lax.broadcasted_iota(jnp.int32, (width_x, rows_y, depth), 1)
    z_ids = lax.broadcasted_iota(jnp.int32, (width_x, rows_y, depth), 2)
    flat_ids = (x_ids * full_y + y_ids) * depth + z_ids
    first = (flat_ids[None] == pairs[:, 0][:, None, None, None]).astype(jnp.float32)
    second = (flat_ids[None] == pairs[:, 1][:, None, None, None]).astype(jnp.float32)
    return CURRENT * first - CURRENT * second


def on_device(potential_init, conductivity, inverse_rows, electrodes, intersection_width):
    local_src, width_x, full_y, depth = potential_init.shape
    n_core = lax.axis_size(CORE)
    n_sub = lax.axis_size("sub")
    core = lax.axis_index(CORE)
    grp_index = (lax.axis_index("xl") * lax.axis_size("y") + lax.axis_index("y")) * n_core + core
    sub_index = lax.axis_index("sub")
    extended = inverse_rows.shape[1]
    rows = inverse_rows.shape[2]
    blocks = full_y // (rows * n_core)
    margin = (extended - width_x) // 2
    rim = margin + 1
    cell_count = float(width_x * n_sub * full_y * depth)
    x_start = sub_index * width_x
    column_ids = jnp.arange(extended, dtype=jnp.int32)
    reach = intersection_width[0]
    column_x = x_start - margin + column_ids
    column_mask = (
        (column_ids >= margin - reach)
        & (column_ids < width_x + margin + reach)
        & (column_x >= 0)
        & (column_x < width_x * n_sub)
    ).astype(jnp.float32)
    inverse_mine = lax.all_gather(inverse_rows, CHIP_AXES, axis=2, tiled=True)

    c_lo, c_hi = rims_of(conductivity, rim, 0)
    conduct_pad = jnp.pad(jnp.concatenate([c_lo, conductivity, c_hi], axis=0), ((0, 0), (1, 1), (1, 1)))
    center_coef, face_coefs = face_terms(conduct_pad)
    y_ids = lax.broadcasted_iota(jnp.int32, center_coef.shape, 1)
    z_ids = lax.broadcasted_iota(jnp.int32, center_coef.shape, 2)
    coefs = [
        center_coef,
        face_coefs[0],
        face_coefs[1],
        jnp.where(y_ids == full_y - 1, 0.0, face_coefs[2]),
        jnp.where(y_ids == 0, 0.0, face_coefs[3]),
        jnp.where(z_ids == depth - 1, 0.0, face_coefs[4]),
        jnp.where(z_ids == 0, 0.0, face_coefs[5]),
    ]
    own_pairs = lax.dynamic_slice_in_dim(electrodes, grp_index * local_src, local_src, 0)
    source_term = source_block(own_pairs, x_start - margin, extended, full_y, full_y, depth)

    mid_planes = list(range(1, width_x - 1))
    bnd_planes = list(range(-margin, 1)) + list(range(width_x - 1, width_x + margin))
    own_planes = list(range(width_x))

    mid_coefs = [c[1 + margin : width_x - 1 + margin] for c in coefs]
    bnd_coefs = [jnp.concatenate([c[: margin + 1], c[width_x - 1 + margin :]], axis=0) for c in coefs]
    own_coefs = [c[margin : margin + width_x] for c in coefs]
    mid_st = source_term[:, 1 + margin : width_x - 1 + margin]
    bnd_st = jnp.concatenate([source_term[:, : margin + 1], source_term[:, width_x - 1 + margin :]], axis=1)
    own_st = source_term[:, margin : margin + width_x]
    mid_coefs, bnd_coefs, own_coefs, mid_st, bnd_st, own_st = lax.optimization_barrier(
        (mid_coefs, bnd_coefs, own_coefs, mid_st, bnd_st, own_st)
    )
    core_vec = jnp.reshape(core, (1,)).astype(jnp.int32)

    columns = []
    for j in range(extended):
        p = j - margin
        if p in mid_planes:
            columns.append((0, mid_planes.index(p)))
        else:
            columns.append((1, bnd_planes.index(p)))

    swap = [(0, 1), (1, 0)]

    potential = potential_init
    for sweep in range(ITERS):
        lo, hi = rims_of(potential, rim, 1)
        mid_own, mid_other = stencil_call(mid_planes, core_vec, potential, [], mid_st, mid_coefs, "split")
        mid_got = lax.ppermute(mid_other, CORE, swap)
        bnd_own, bnd_other = stencil_call(bnd_planes, core_vec, potential, [lo, hi], bnd_st, bnd_coefs, "split")
        bnd_got = lax.ppermute(bnd_other, CORE, swap)
        correction = correction_call(
            column_mask, inverse_mine, [mid_own, bnd_own], [mid_got, bnd_got], columns
        ).reshape(2 * local_src, width_x, blocks, rows, depth)
        mine = correction[:local_src]
        back = lax.ppermute(correction[local_src:], CORE, swap)
        first = jnp.where(core == 0, mine, back)
        second = jnp.where(core == 0, back, mine)
        update = jnp.stack([first, second], axis=3).reshape(potential.shape)
        potential = potential + update
    lo, hi = rims_of(potential, 1, 1)
    squares = stencil_call(own_planes, core_vec, potential, [lo, hi], own_st, own_coefs, "norm")
    totals = lax.psum(jnp.sum(squares, axis=(1, 2)), "sub")
    residual_norms = jnp.sqrt(totals / cell_count)
    return (potential, residual_norms)


def solution(mesh):
    n_sub, n_grp = mesh.devices.shape
    n_core = 2
    n_y = 4
    view = Mesh(
        mesh.devices.reshape(n_sub, n_grp // (n_y * n_core), n_y, n_core),
        ("sub", "xl", "y", "core"),
    )
    in_specs = (
        P(GRP, "sub", None, None),
        P("sub", None, None),
        P("sub", None, GRP, None),
        P(),
        P("sub"),
    )
    out_specs = (P(GRP, "sub", None, None), P(GRP))
    return jax.shard_map(
        on_device, mesh=view, in_specs=in_specs, out_specs=out_specs, check_vma=False
    )
```

```python
import jax
import jax.numpy as jnp
from jax import lax
from jax.sharding import Mesh, PartitionSpec as P
from jax.experimental import pallas as pl
from jax.experimental.pallas import tpu as pltpu

ITERS = 2
INTERPRET = False

CURRENT = 16.0
MASS = 1.0

CHIP_AXES = ("xl", "y")
CORE = "core"
GRP = ("xl", "y", "core")


def make_stencil_kernel(planes, has_rim, mode, n_after):
    def kernel(core_ref, *refs):
        n_in = 3 if has_rim else 1
        v_ref = refs[0]
        lo_ref, hi_ref = (refs[1], refs[2]) if has_rim else (None, None)
        st_ref, cc_ref, fxp_ref, fxm_ref, fyp_ref, fym_ref, fzp_ref, fzm_ref = refs[n_in : n_in + 8]
        outs = refs[n_in + 8 + n_after :]
        width = v_ref.shape[1]
        ny, nz = v_ref.shape[2], v_ref.shape[3]
        core = core_ref[0]

        def load(q):
            if q < 0:
                return lo_ref[0, lo_ref.shape[1] + q]
            if q >= width:
                return hi_ref[0, q - width]
            return v_ref[0, q]

        total = None
        for o, p in enumerate(planes):
            v = load(p)
            image = cc_ref[o] * v
            image = image - fxp_ref[o] * load(p + 1)
            image = image - fxm_ref[o] * load(p - 1)
            image = image - fyp_ref[o] * pltpu.roll(v, ny - 1, 0)
            image = image - fym_ref[o] * pltpu.roll(v, 1, 0)
            image = image - fzp_ref[o] * pltpu.roll(v, nz - 1, 1)
            image = image - fzm_ref[o] * pltpu.roll(v, 1, 1)
            resid = st_ref[0, o] - image
            if mode == "norm":
                square = resid * resid
                total = square if total is None else total + square
                continue
            own_ref, other_ref = outs
            tile = 8
            for g in range(ny // (2 * tile)):
                first = resid[2 * g * tile : (2 * g + 1) * tile]
                second = resid[(2 * g + 1) * tile : (2 * g + 2) * tile]
                own_ref[0, o, g * tile : (g + 1) * tile] = jnp.where(core == 0, first, second)
                other_ref[0, o, g * tile : (g + 1) * tile] = jnp.where(core == 0, second, first)
        if mode == "norm":
            outs[0][0] = total.reshape(ny // 8, 8, nz).sum(axis=0)

    return kernel


def stencil_call(planes, core, v, rims, st, coefs, mode, after=()):
    n_src, width, ny, nz = v.shape
    n_out = len(planes)
    own_block = pl.BlockSpec((1, width, ny, nz), lambda s: (s, 0, 0, 0))
    st_block = pl.BlockSpec((1, n_out, ny, nz), lambda s: (s, 0, 0, 0))
    coef_block = pl.BlockSpec((n_out, ny, nz), lambda s: (0, 0, 0))
    rim_specs = [pl.BlockSpec((1, r.shape[1], ny, nz), lambda s: (s, 0, 0, 0)) for r in rims]
    if mode == "norm":
        out_specs = pl.BlockSpec((1, 8, nz), lambda s: (s, 0, 0))
        out_shape = jax.ShapeDtypeStruct((n_src, 8, nz), jnp.float32)
    else:
        half = pl.BlockSpec((1, n_out, ny // 2, nz), lambda s: (s, 0, 0, 0))
        out_specs = [half, half]
        out_shape = [jax.ShapeDtypeStruct((n_src, n_out, ny // 2, nz), jnp.float32)] * 2
    return pl.pallas_call(
        make_stencil_kernel(tuple(planes), len(rims) > 0, mode, len(after)),
        grid=(n_src,),
        in_specs=[pl.BlockSpec(memory_space=pltpu.SMEM), own_block] + rim_specs + [st_block] + [coef_block] * 7
        + [pl.BlockSpec(memory_space=pl.ANY)] * len(after),
        out_specs=out_specs,
        out_shape=out_shape,
        interpret=INTERPRET,
    )(core, v, *rims, st, *coefs, *after)


def make_correction_kernel(columns, has_partial):
    def kernel(mask_ref, inv_ref, *refs):
        out_ref = refs[-1]
        partial_ref = refs[-2] if has_partial else None
        pieces = refs[: len(refs) - (2 if has_partial else 1)]
        n_out = inv_ref.shape[0]
        halves = len(pieces) // 2

        def row(i, carry):
            accs = None
            for j, piece, plane in columns:
                w = inv_ref[i, j] * mask_ref[j]
                terms = []
                for half in range(2):
                    src_ref = pieces[half * halves + piece]
                    for s in range(src_ref.shape[0]):
                        terms.append(w * src_ref[s, plane])
                accs = terms if accs is None else [a + t for a, t in zip(accs, terms)]
            for s, acc in enumerate(accs):
                if has_partial:
                    acc = partial_ref[s, i] + acc
                out_ref[s, i] = acc
            return carry

        lax.fori_loop(0, n_out, row, 0)

    return kernel


def correction_call(mask, inv, own_pieces, got_pieces, columns, partial=None, rows=8):
    n_out, n_col, ny, nz = inv.shape
    n_src = own_pieces[0].shape[0] * 2
    specs = [pl.BlockSpec((p.shape[0], p.shape[1], rows, nz), lambda b: (0, 0, b, 0)) for p in own_pieces + got_pieces]
    out_spec = pl.BlockSpec((n_src, n_out, rows, nz), lambda b: (0, 0, b, 0))
    extra = [] if partial is None else [partial]
    return pl.pallas_call(
        make_correction_kernel(tuple(columns), partial is not None),
        grid=(ny // rows,),
        in_specs=[pl.BlockSpec(memory_space=pltpu.SMEM),
                  pl.BlockSpec((n_out, n_col, rows, nz), lambda b: (0, 0, b, 0))] + specs + [out_spec] * len(extra),
        out_specs=out_spec,
        out_shape=jax.ShapeDtypeStruct((n_src, n_out, ny, nz), jnp.float32),
        interpret=INTERPRET,
    )(mask, inv, *own_pieces, *got_pieces, *extra)


def rims_of(cells, depth_x, dim):
    count = lax.axis_size("sub")
    head = lax.slice_in_dim(cells, 0, depth_x, axis=dim)
    tail = lax.slice_in_dim(cells, cells.shape[dim] - depth_x, cells.shape[dim], axis=dim)
    lo = lax.ppermute(tail, "sub", [(i, i + 1) for i in range(count - 1)])
    hi = lax.ppermute(head, "sub", [(i + 1, i) for i in range(count - 1)])
    return lo, hi


def neighbours(padded):
    return [
        padded[..., 2:, 1:-1, 1:-1],
        padded[..., :-2, 1:-1, 1:-1],
        padded[..., 1:-1, 2:, 1:-1],
        padded[..., 1:-1, :-2, 1:-1],
        padded[..., 1:-1, 1:-1, 2:],
        padded[..., 1:-1, 1:-1, :-2],
    ]


def face_terms(conduct_pad):
    center_cells = conduct_pad[1:-1, 1:-1, 1:-1]
    face_coefs = [0.5 * (center_cells + beside_cell) for beside_cell in neighbours(conduct_pad)]
    center_coef = MASS * center_cells
    for face_coef in face_coefs:
        center_coef = center_coef + face_coef
    return (center_coef, face_coefs)


def source_block(pairs, x_start, width_x, rows_y, full_y, depth):
    x_ids = x_start + lax.broadcasted_iota(jnp.int32, (width_x, rows_y, depth), 0)
    y_ids = lax.broadcasted_iota(jnp.int32, (width_x, rows_y, depth), 1)
    z_ids = lax.broadcasted_iota(jnp.int32, (width_x, rows_y, depth), 2)
    flat_ids = (x_ids * full_y + y_ids) * depth + z_ids
    first = (flat_ids[None] == pairs[:, 0][:, None, None, None]).astype(jnp.float32)
    second = (flat_ids[None] == pairs[:, 1][:, None, None, None]).astype(jnp.float32)
    return CURRENT * first - CURRENT * second


def on_device(potential_init, conductivity, inverse_rows, electrodes, intersection_width):
    local_src, width_x, full_y, depth = potential_init.shape
    n_core = lax.axis_size(CORE)
    n_sub = lax.axis_size("sub")
    core = lax.axis_index(CORE)
    grp_index = (lax.axis_index("xl") * lax.axis_size("y") + lax.axis_index("y")) * n_core + core
    sub_index = lax.axis_index("sub")
    extended = inverse_rows.shape[1]
    rows = inverse_rows.shape[2]
    blocks = full_y // (rows * n_core)
    margin = (extended - width_x) // 2
    rim = margin + 1
    cell_count = float(width_x * n_sub * full_y * depth)
    x_start = sub_index * width_x
    column_ids = jnp.arange(extended, dtype=jnp.int32)
    reach = intersection_width[0]
    column_x = x_start - margin + column_ids
    column_mask = (
        (column_ids >= margin - reach)
        & (column_ids < width_x + margin + reach)
        & (column_x >= 0)
        & (column_x < width_x * n_sub)
    ).astype(jnp.float32)
    inverse_mine = lax.all_gather(inverse_rows, CHIP_AXES, axis=2, tiled=True)

    c_lo, c_hi = rims_of(conductivity, rim, 0)
    conduct_pad = jnp.pad(jnp.concatenate([c_lo, conductivity, c_hi], axis=0), ((0, 0), (1, 1), (1, 1)))
    center_coef, face_coefs = face_terms(conduct_pad)
    y_ids = lax.broadcasted_iota(jnp.int32, center_coef.shape, 1)
    z_ids = lax.broadcasted_iota(jnp.int32, center_coef.shape, 2)
    coefs = [
        center_coef,
        face_coefs[0],
        face_coefs[1],
        jnp.where(y_ids == full_y - 1, 0.0, face_coefs[2]),
        jnp.where(y_ids == 0, 0.0, face_coefs[3]),
        jnp.where(z_ids == depth - 1, 0.0, face_coefs[4]),
        jnp.where(z_ids == 0, 0.0, face_coefs[5]),
    ]
    own_pairs = lax.dynamic_slice_in_dim(electrodes, grp_index * local_src, local_src, 0)
    source_term = source_block(own_pairs, x_start - margin, extended, full_y, full_y, depth)

    mid_planes = list(range(1, width_x - 1))
    bnd_planes = list(range(-margin, 1)) + list(range(width_x - 1, width_x + margin))

    mid_coefs = [c[1 + margin : width_x - 1 + margin] for c in coefs]
    bnd_coefs = [jnp.concatenate([c[: margin + 1], c[width_x - 1 + margin :]], axis=0) for c in coefs]
    edge_planes = [0, width_x - 1]
    edge_coefs = [jnp.concatenate([c[margin : margin + 1], c[margin + width_x - 1 : margin + width_x]], axis=0) for c in coefs]
    edge_st = jnp.concatenate(
        [source_term[:, margin : margin + 1], source_term[:, margin + width_x - 1 : margin + width_x]], axis=1)
    mid_st = source_term[:, 1 + margin : width_x - 1 + margin]
    bnd_st = jnp.concatenate([source_term[:, : margin + 1], source_term[:, width_x - 1 + margin :]], axis=1)
    mid_coefs, bnd_coefs, edge_coefs, mid_st, bnd_st, edge_st = lax.optimization_barrier(
        (mid_coefs, bnd_coefs, edge_coefs, mid_st, bnd_st, edge_st)
    )
    core_vec = jnp.reshape(core, (1,)).astype(jnp.int32)

    mid_columns = [(j, 0, mid_planes.index(j - margin)) for j in range(extended) if j - margin in mid_planes]
    bnd_columns = [(j, 0, bnd_planes.index(j - margin)) for j in range(extended) if j - margin in bnd_planes]

    swap = [(0, 1), (1, 0)]

    potential = potential_init
    for sweep in range(ITERS):
      lo, hi = rims_of(potential, rim, 1)
      mid_own, mid_other = stencil_call(mid_planes, core_vec, potential, [], mid_st, mid_coefs, "split")
      mid_got = lax.ppermute(mid_other, CORE, swap)
      inner = correction_call(column_mask, inverse_mine, [mid_own], [mid_got], mid_columns)
      after = (inner,) if sweep > 0 else ()
      bnd_own, bnd_other = stencil_call(
          bnd_planes, core_vec, potential, [lo, hi], bnd_st, bnd_coefs, "split", after=after)
      bnd_got = lax.ppermute(bnd_other, CORE, swap)
      correction = correction_call(
          column_mask, inverse_mine, [bnd_own], [bnd_got], bnd_columns, partial=inner
      ).reshape(2 * local_src, width_x, blocks, rows, depth)
      mine = correction[:local_src]
      back = lax.ppermute(correction[local_src:], CORE, swap)
      first = jnp.where(core == 0, mine, back)
      second = jnp.where(core == 0, back, mine)
      update = jnp.stack([first, second], axis=3).reshape(potential.shape)
      potential = potential + update
    lo, hi = rims_of(potential, 1, 1)
    inner_squares = stencil_call(mid_planes, core_vec, potential, [], mid_st, mid_coefs, "norm")
    rim_squares = stencil_call(edge_planes, core_vec, potential, [lo, hi], edge_st, edge_coefs, "norm")
    totals = lax.psum(jnp.sum(inner_squares + rim_squares, axis=(1, 2)), "sub")
    residual_norms = jnp.sqrt(totals / cell_count)
    return (potential, residual_norms)


def solution(mesh):
    n_sub, n_grp = mesh.devices.shape
    n_core = 2
    n_y = 4
    view = Mesh(
        mesh.devices.reshape(n_sub, n_grp // (n_y * n_core), n_y, n_core),
        ("sub", "xl", "y", "core"),
    )
    in_specs = (
        P(GRP, "sub", None, None),
        P("sub", None, None),
        P("sub", None, GRP, None),
        P(),
        P("sub"),
    )
    out_specs = (P(GRP, "sub", None, None), P(GRP))
    return jax.shard_map(
        on_device, mesh=view, in_specs=in_specs, out_specs=out_specs, check_vma=False
    )
```

```python
import jax
import jax.numpy as jnp
from jax import lax
from jax.sharding import Mesh, PartitionSpec as P
from jax.experimental import pallas as pl
from jax.experimental.pallas import tpu as pltpu

ITERS = 2
INTERPRET = False

CURRENT = 16.0
MASS = 1.0

CHIP_AXES = ("xl", "y")
CORE = "core"
GRP = ("xl", "y", "core")


def make_stencil_kernel(planes, has_rim, mode, n_after):
    def kernel(core_ref, *refs):
        n_in = 3 if has_rim else 1
        v_ref = refs[0]
        lo_ref, hi_ref = (refs[1], refs[2]) if has_rim else (None, None)
        st_ref, cc_ref, fxp_ref, fxm_ref, fyp_ref, fym_ref, fzp_ref, fzm_ref = refs[n_in : n_in + 8]
        outs = refs[n_in + 8 + n_after :]
        width = v_ref.shape[1]
        ny, nz = v_ref.shape[2], v_ref.shape[3]
        core = core_ref[0]

        def load(q):
            if q < 0:
                return lo_ref[0, lo_ref.shape[1] + q]
            if q >= width:
                return hi_ref[0, q - width]
            return v_ref[0, q]

        total = None
        for o, p in enumerate(planes):
            v = load(p)
            image = cc_ref[o] * v
            image = image - fxp_ref[o] * load(p + 1)
            image = image - fxm_ref[o] * load(p - 1)
            image = image - fyp_ref[o] * pltpu.roll(v, ny - 1, 0)
            image = image - fym_ref[o] * pltpu.roll(v, 1, 0)
            image = image - fzp_ref[o] * pltpu.roll(v, nz - 1, 1)
            image = image - fzm_ref[o] * pltpu.roll(v, 1, 1)
            resid = st_ref[0, o] - image
            if mode == "norm":
                square = resid * resid
                total = square if total is None else total + square
                continue
            own_ref, other_ref = outs
            tile = 8
            for g in range(ny // (2 * tile)):
                first = resid[2 * g * tile : (2 * g + 1) * tile]
                second = resid[(2 * g + 1) * tile : (2 * g + 2) * tile]
                own_ref[0, o, g * tile : (g + 1) * tile] = jnp.where(core == 0, first, second)
                other_ref[0, o, g * tile : (g + 1) * tile] = jnp.where(core == 0, second, first)
        if mode == "norm":
            outs[0][0] = total.reshape(ny // 8, 8, nz).sum(axis=0)

    return kernel


def stencil_call(planes, core, v, rims, st, coefs, mode, after=()):
    n_src, width, ny, nz = v.shape
    n_out = len(planes)
    own_block = pl.BlockSpec((1, width, ny, nz), lambda s: (s, 0, 0, 0))
    st_block = pl.BlockSpec((1, n_out, ny, nz), lambda s: (s, 0, 0, 0))
    coef_block = pl.BlockSpec((n_out, ny, nz), lambda s: (0, 0, 0))
    rim_specs = [pl.BlockSpec((1, r.shape[1], ny, nz), lambda s: (s, 0, 0, 0)) for r in rims]
    if mode == "norm":
        out_specs = pl.BlockSpec((1, 8, nz), lambda s: (s, 0, 0))
        out_shape = jax.ShapeDtypeStruct((n_src, 8, nz), jnp.float32)
    else:
        half = pl.BlockSpec((1, n_out, ny // 2, nz), lambda s: (s, 0, 0, 0))
        out_specs = [half, half]
        out_shape = [jax.ShapeDtypeStruct((n_src, n_out, ny // 2, nz), jnp.float32)] * 2
    return pl.pallas_call(
        make_stencil_kernel(tuple(planes), len(rims) > 0, mode, len(after)),
        grid=(n_src,),
        in_specs=[pl.BlockSpec(memory_space=pltpu.SMEM), own_block] + rim_specs + [st_block] + [coef_block] * 7
        + [pl.BlockSpec(memory_space=pl.ANY)] * len(after),
        out_specs=out_specs,
        out_shape=out_shape,
        interpret=INTERPRET,
    )(core, v, *rims, st, *coefs, *after)


def make_correction_kernel(columns, has_partial):
    def kernel(mask_ref, inv_ref, *refs):
        out_ref = refs[-1]
        partial_ref = refs[-2] if has_partial else None
        pieces = refs[: len(refs) - (2 if has_partial else 1)]
        n_out = inv_ref.shape[0]
        halves = len(pieces) // 2

        def row(i, carry):
            accs = None
            for j, col, piece, plane in columns:
                w = inv_ref[i, col] * mask_ref[j]
                terms = []
                for half in range(2):
                    src_ref = pieces[half * halves + piece]
                    for s in range(src_ref.shape[0]):
                        terms.append(w * src_ref[s, plane])
                accs = terms if accs is None else [a + t for a, t in zip(accs, terms)]
            for s, acc in enumerate(accs):
                if has_partial:
                    acc = partial_ref[s, i] + acc
                out_ref[s, i] = acc
            return carry

        lax.fori_loop(0, n_out, row, 0)

    return kernel


def correction_call(mask, inv, own_pieces, got_pieces, columns, partial=None, rows=8):
    n_out, n_col, ny, nz = inv.shape
    n_src = own_pieces[0].shape[0] * 2
    specs = [pl.BlockSpec((p.shape[0], p.shape[1], rows, nz), lambda b: (0, 0, b, 0)) for p in own_pieces + got_pieces]
    out_spec = pl.BlockSpec((n_src, n_out, rows, nz), lambda b: (0, 0, b, 0))
    extra = [] if partial is None else [partial]
    return pl.pallas_call(
        make_correction_kernel(tuple(columns), partial is not None),
        grid=(ny // rows,),
        in_specs=[pl.BlockSpec(memory_space=pltpu.SMEM),
                  pl.BlockSpec((n_out, n_col, rows, nz), lambda b: (0, 0, b, 0))] + specs + [out_spec] * len(extra),
        out_specs=out_spec,
        out_shape=jax.ShapeDtypeStruct((n_src, n_out, ny, nz), jnp.float32),
        interpret=INTERPRET,
    )(mask, inv, *own_pieces, *got_pieces, *extra)


def rims_of(cells, depth_x, dim):
    count = lax.axis_size("sub")
    head = lax.slice_in_dim(cells, 0, depth_x, axis=dim)
    tail = lax.slice_in_dim(cells, cells.shape[dim] - depth_x, cells.shape[dim], axis=dim)
    lo = lax.ppermute(tail, "sub", [(i, i + 1) for i in range(count - 1)])
    hi = lax.ppermute(head, "sub", [(i + 1, i) for i in range(count - 1)])
    return lo, hi


def neighbours(padded):
    return [
        padded[..., 2:, 1:-1, 1:-1],
        padded[..., :-2, 1:-1, 1:-1],
        padded[..., 1:-1, 2:, 1:-1],
        padded[..., 1:-1, :-2, 1:-1],
        padded[..., 1:-1, 1:-1, 2:],
        padded[..., 1:-1, 1:-1, :-2],
    ]


def face_terms(conduct_pad):
    center_cells = conduct_pad[1:-1, 1:-1, 1:-1]
    face_coefs = [0.5 * (center_cells + beside_cell) for beside_cell in neighbours(conduct_pad)]
    center_coef = MASS * center_cells
    for face_coef in face_coefs:
        center_coef = center_coef + face_coef
    return (center_coef, face_coefs)


def source_block(pairs, x_start, width_x, rows_y, full_y, depth):
    x_ids = x_start + lax.broadcasted_iota(jnp.int32, (width_x, rows_y, depth), 0)
    y_ids = lax.broadcasted_iota(jnp.int32, (width_x, rows_y, depth), 1)
    z_ids = lax.broadcasted_iota(jnp.int32, (width_x, rows_y, depth), 2)
    flat_ids = (x_ids * full_y + y_ids) * depth + z_ids
    first = (flat_ids[None] == pairs[:, 0][:, None, None, None]).astype(jnp.float32)
    second = (flat_ids[None] == pairs[:, 1][:, None, None, None]).astype(jnp.float32)
    return CURRENT * first - CURRENT * second


def on_device(potential_init, conductivity, inverse_rows, electrodes, intersection_width):
    local_src, width_x, full_y, depth = potential_init.shape
    n_core = lax.axis_size(CORE)
    n_sub = lax.axis_size("sub")
    core = lax.axis_index(CORE)
    grp_index = (lax.axis_index("xl") * lax.axis_size("y") + lax.axis_index("y")) * n_core + core
    sub_index = lax.axis_index("sub")
    extended = inverse_rows.shape[1]
    rows = inverse_rows.shape[2]
    blocks = full_y // (rows * n_core)
    margin = (extended - width_x) // 2
    rim = margin + 1
    cell_count = float(width_x * n_sub * full_y * depth)
    x_start = sub_index * width_x
    column_ids = jnp.arange(extended, dtype=jnp.int32)
    reach = intersection_width[0]
    column_x = x_start - margin + column_ids
    column_mask = (
        (column_ids >= margin - reach)
        & (column_ids < width_x + margin + reach)
        & (column_x >= 0)
        & (column_x < width_x * n_sub)
    ).astype(jnp.float32)
    inner_cols = list(range(margin + 1, margin + width_x - 1))
    rim_cols = list(range(0, margin + 1)) + list(range(margin + width_x - 1, extended))
    inverse_inner = lax.all_gather(
        inverse_rows[:, inner_cols[0] : inner_cols[-1] + 1], CHIP_AXES, axis=2, tiled=True)
    inverse_rim = lax.all_gather(
        jnp.concatenate([inverse_rows[:, : margin + 1], inverse_rows[:, margin + width_x - 1 :]], axis=1),
        CHIP_AXES, axis=2, tiled=True)

    c_lo, c_hi = rims_of(conductivity, rim, 0)
    conduct_pad = jnp.pad(jnp.concatenate([c_lo, conductivity, c_hi], axis=0), ((0, 0), (1, 1), (1, 1)))
    center_coef, face_coefs = face_terms(conduct_pad)
    y_ids = lax.broadcasted_iota(jnp.int32, center_coef.shape, 1)
    z_ids = lax.broadcasted_iota(jnp.int32, center_coef.shape, 2)
    coefs = [
        center_coef,
        face_coefs[0],
        face_coefs[1],
        jnp.where(y_ids == full_y - 1, 0.0, face_coefs[2]),
        jnp.where(y_ids == 0, 0.0, face_coefs[3]),
        jnp.where(z_ids == depth - 1, 0.0, face_coefs[4]),
        jnp.where(z_ids == 0, 0.0, face_coefs[5]),
    ]
    own_pairs = lax.dynamic_slice_in_dim(electrodes, grp_index * local_src, local_src, 0)
    source_term = source_block(own_pairs, x_start - margin, extended, full_y, full_y, depth)

    mid_planes = list(range(1, width_x - 1))
    bnd_planes = list(range(-margin, 1)) + list(range(width_x - 1, width_x + margin))

    mid_coefs = [c[1 + margin : width_x - 1 + margin] for c in coefs]
    bnd_coefs = [jnp.concatenate([c[: margin + 1], c[width_x - 1 + margin :]], axis=0) for c in coefs]
    edge_planes = [0, width_x - 1]
    edge_coefs = [jnp.concatenate([c[margin : margin + 1], c[margin + width_x - 1 : margin + width_x]], axis=0) for c in coefs]
    edge_st = jnp.concatenate(
        [source_term[:, margin : margin + 1], source_term[:, margin + width_x - 1 : margin + width_x]], axis=1)
    mid_st = source_term[:, 1 + margin : width_x - 1 + margin]
    bnd_st = jnp.concatenate([source_term[:, : margin + 1], source_term[:, width_x - 1 + margin :]], axis=1)
    mid_coefs, bnd_coefs, edge_coefs, mid_st, bnd_st, edge_st = lax.optimization_barrier(
        (mid_coefs, bnd_coefs, edge_coefs, mid_st, bnd_st, edge_st)
    )
    core_vec = jnp.reshape(core, (1,)).astype(jnp.int32)

    mid_columns = [(j, inner_cols.index(j), 0, mid_planes.index(j - margin)) for j in inner_cols]
    bnd_columns = [(j, rim_cols.index(j), 0, bnd_planes.index(j - margin)) for j in rim_cols]

    swap = [(0, 1), (1, 0)]

    potential = potential_init
    for sweep in range(ITERS):
      lo, hi = rims_of(potential, rim, 1)
      mid_own, mid_other = stencil_call(mid_planes, core_vec, potential, [], mid_st, mid_coefs, "split")
      mid_got = lax.ppermute(mid_other, CORE, swap)
      inner = correction_call(column_mask, inverse_inner, [mid_own], [mid_got], mid_columns)
      after = (inner,) if sweep > 0 else ()
      bnd_own, bnd_other = stencil_call(
          bnd_planes, core_vec, potential, [lo, hi], bnd_st, bnd_coefs, "split", after=after)
      bnd_got = lax.ppermute(bnd_other, CORE, swap)
      correction = correction_call(
          column_mask, inverse_rim, [bnd_own], [bnd_got], bnd_columns, partial=inner
      ).reshape(2 * local_src, width_x, blocks, rows, depth)
      mine = correction[:local_src]
      back = lax.ppermute(correction[local_src:], CORE, swap)
      first = jnp.where(core == 0, mine, back)
      second = jnp.where(core == 0, back, mine)
      update = jnp.stack([first, second], axis=3).reshape(potential.shape)
      potential = potential + update
    lo, hi = rims_of(potential, 1, 1)
    inner_squares = stencil_call(mid_planes, core_vec, potential, [], mid_st, mid_coefs, "norm")
    rim_squares = stencil_call(edge_planes, core_vec, potential, [lo, hi], edge_st, edge_coefs, "norm")
    totals = lax.psum(jnp.sum(inner_squares + rim_squares, axis=(1, 2)), "sub")
    residual_norms = jnp.sqrt(totals / cell_count)
    return (potential, residual_norms)


def solution(mesh):
    n_sub, n_grp = mesh.devices.shape
    n_core = 2
    n_y = 4
    view = Mesh(
        mesh.devices.reshape(n_sub, n_grp // (n_y * n_core), n_y, n_core),
        ("sub", "xl", "y", "core"),
    )
    in_specs = (
        P(GRP, "sub", None, None),
        P("sub", None, None),
        P("sub", None, GRP, None),
        P(),
        P("sub"),
    )
    out_specs = (P(GRP, "sub", None, None), P(GRP))
    return jax.shard_map(
        on_device, mesh=view, in_specs=in_specs, out_specs=out_specs, check_vma=False
    )
```

```python
import jax
import jax.numpy as jnp
from jax import lax
from jax.sharding import Mesh, PartitionSpec as P
from jax.experimental import pallas as pl
from jax.experimental.pallas import tpu as pltpu

ITERS = 2
INTERPRET = False

CURRENT = 16.0
MASS = 1.0

CHIP_AXES = ("xl", "y")
CORE = "core"
GRP = ("xl", "y", "core")


def make_stencil_kernel(planes, has_rim, mode):
    def kernel(core_ref, *refs):
        n_in = 3 if has_rim else 1
        v_ref = refs[0]
        lo_ref, hi_ref = (refs[1], refs[2]) if has_rim else (None, None)
        st_ref, cc_ref, fxp_ref, fxm_ref, fyp_ref, fym_ref, fzp_ref, fzm_ref = refs[n_in : n_in + 8]
        outs = refs[n_in + 8 :]
        width = v_ref.shape[1]
        ny, nz = v_ref.shape[2], v_ref.shape[3]
        core = core_ref[0]

        def load(q):
            if q < 0:
                return lo_ref[0, lo_ref.shape[1] + q]
            if q >= width:
                return hi_ref[0, q - width]
            return v_ref[0, q]

        total = None
        for o, p in enumerate(planes):
            v = load(p)
            image = cc_ref[o] * v
            image = image - fxp_ref[o] * load(p + 1)
            image = image - fxm_ref[o] * load(p - 1)
            image = image - fyp_ref[o] * pltpu.roll(v, ny - 1, 0)
            image = image - fym_ref[o] * pltpu.roll(v, 1, 0)
            image = image - fzp_ref[o] * pltpu.roll(v, nz - 1, 1)
            image = image - fzm_ref[o] * pltpu.roll(v, 1, 1)
            resid = st_ref[0, o] - image
            if mode == "norm":
                square = resid * resid
                total = square if total is None else total + square
                continue
            own_ref, other_ref = outs
            tile = 8
            for g in range(ny // (2 * tile)):
                first = resid[2 * g * tile : (2 * g + 1) * tile]
                second = resid[(2 * g + 1) * tile : (2 * g + 2) * tile]
                own_ref[0, o, g * tile : (g + 1) * tile] = jnp.where(core == 0, first, second)
                other_ref[0, o, g * tile : (g + 1) * tile] = jnp.where(core == 0, second, first)
        if mode == "norm":
            outs[0][0] = total.reshape(ny // 8, 8, nz).sum(axis=0)

    return kernel


def stencil_call(planes, core, v, rims, st, coefs, mode):
    n_src, width, ny, nz = v.shape
    n_out = len(planes)
    own_block = pl.BlockSpec((1, width, ny, nz), lambda s: (s, 0, 0, 0))
    st_block = pl.BlockSpec((1, n_out, ny, nz), lambda s: (s, 0, 0, 0))
    coef_block = pl.BlockSpec((n_out, ny, nz), lambda s: (0, 0, 0))
    rim_specs = [pl.BlockSpec((1, r.shape[1], ny, nz), lambda s: (s, 0, 0, 0)) for r in rims]
    if mode == "norm":
        out_specs = pl.BlockSpec((1, 8, nz), lambda s: (s, 0, 0))
        out_shape = jax.ShapeDtypeStruct((n_src, 8, nz), jnp.float32)
    else:
        half = pl.BlockSpec((1, n_out, ny // 2, nz), lambda s: (s, 0, 0, 0))
        out_specs = [half, half]
        out_shape = [jax.ShapeDtypeStruct((n_src, n_out, ny // 2, nz), jnp.float32)] * 2
    return pl.pallas_call(
        make_stencil_kernel(tuple(planes), len(rims) > 0, mode),
        grid=(n_src,),
        in_specs=[pl.BlockSpec(memory_space=pltpu.SMEM), own_block] + rim_specs + [st_block] + [coef_block] * 7,
        out_specs=out_specs,
        out_shape=out_shape,
        interpret=INTERPRET,
    )(core, v, *rims, st, *coefs)


def make_correction_kernel(columns):
    def kernel(mask_ref, inv_ref, *refs):
        out_ref = refs[-1]
        pieces = refs[:-1]
        n_out = inv_ref.shape[0]
        halves = len(pieces) // 2

        def row(i, carry):
            accs = None
            for j, (piece, plane) in enumerate(columns):
                w = inv_ref[i, j] * mask_ref[j]
                terms = []
                for half in range(2):
                    src_ref = pieces[half * halves + piece]
                    for s in range(src_ref.shape[0]):
                        terms.append(w * src_ref[s, plane])
                accs = terms if accs is None else [a + t for a, t in zip(accs, terms)]
            for s, acc in enumerate(accs):
                out_ref[s, i] = acc
            return carry

        lax.fori_loop(0, n_out, row, 0)

    return kernel


def correction_call(mask, inv, own_pieces, got_pieces, columns, rows=8):
    n_out, n_col, ny, nz = inv.shape
    n_src = sum(p.shape[0] for p in own_pieces[:1]) * 2
    specs = [pl.BlockSpec((p.shape[0], p.shape[1], rows, nz), lambda b: (0, 0, b, 0)) for p in own_pieces + got_pieces]
    return pl.pallas_call(
        make_correction_kernel(tuple(columns)),
        grid=(ny // rows,),
        in_specs=[pl.BlockSpec(memory_space=pltpu.SMEM),
                  pl.BlockSpec((n_out, n_col, rows, nz), lambda b: (0, 0, b, 0))] + specs,
        out_specs=pl.BlockSpec((n_src, n_out, rows, nz), lambda b: (0, 0, b, 0)),
        out_shape=jax.ShapeDtypeStruct((n_src, n_out, ny, nz), jnp.float32),
        interpret=INTERPRET,
    )(mask, inv, *own_pieces, *got_pieces)


def rims_of(cells, depth_x, dim):
    count = lax.axis_size("sub")
    head = lax.slice_in_dim(cells, 0, depth_x, axis=dim)
    tail = lax.slice_in_dim(cells, cells.shape[dim] - depth_x, cells.shape[dim], axis=dim)
    lo = lax.ppermute(tail, "sub", [(i, i + 1) for i in range(count - 1)])
    hi = lax.ppermute(head, "sub", [(i + 1, i) for i in range(count - 1)])
    return lo, hi


def neighbours(padded):
    return [
        padded[..., 2:, 1:-1, 1:-1],
        padded[..., :-2, 1:-1, 1:-1],
        padded[..., 1:-1, 2:, 1:-1],
        padded[..., 1:-1, :-2, 1:-1],
        padded[..., 1:-1, 1:-1, 2:],
        padded[..., 1:-1, 1:-1, :-2],
    ]


def face_terms(conduct_pad):
    center_cells = conduct_pad[1:-1, 1:-1, 1:-1]
    face_coefs = [0.5 * (center_cells + beside_cell) for beside_cell in neighbours(conduct_pad)]
    center_coef = MASS * center_cells
    for face_coef in face_coefs:
        center_coef = center_coef + face_coef
    return (center_coef, face_coefs)


def source_block(pairs, x_start, width_x, rows_y, full_y, depth):
    x_ids = x_start + lax.broadcasted_iota(jnp.int32, (width_x, rows_y, depth), 0)
    y_ids = lax.broadcasted_iota(jnp.int32, (width_x, rows_y, depth), 1)
    z_ids = lax.broadcasted_iota(jnp.int32, (width_x, rows_y, depth), 2)
    flat_ids = (x_ids * full_y + y_ids) * depth + z_ids
    first = (flat_ids[None] == pairs[:, 0][:, None, None, None]).astype(jnp.float32)
    second = (flat_ids[None] == pairs[:, 1][:, None, None, None]).astype(jnp.float32)
    return CURRENT * first - CURRENT * second


def on_device(potential_init, conductivity, inverse_rows, electrodes, intersection_width):
    local_src, width_x, full_y, depth = potential_init.shape
    n_core = lax.axis_size(CORE)
    n_sub = lax.axis_size("sub")
    core = lax.axis_index(CORE)
    grp_index = (lax.axis_index("xl") * lax.axis_size("y") + lax.axis_index("y")) * n_core + core
    sub_index = lax.axis_index("sub")
    extended = inverse_rows.shape[1]
    rows = inverse_rows.shape[2]
    blocks = full_y // (rows * n_core)
    margin = (extended - width_x) // 2
    rim = margin + 1
    cell_count = float(width_x * n_sub * full_y * depth)
    x_start = sub_index * width_x
    column_ids = jnp.arange(extended, dtype=jnp.int32)
    reach = intersection_width[0]
    column_x = x_start - margin + column_ids
    column_mask = (
        (column_ids >= margin - reach)
        & (column_ids < width_x + margin + reach)
        & (column_x >= 0)
        & (column_x < width_x * n_sub)
    ).astype(jnp.float32)
    c_lo, c_hi = rims_of(conductivity, rim, 0)
    first_lo, first_hi = rims_of(potential_init, rim, 1)
    inverse_rows, c_lo, c_hi, first_lo, first_hi = lax.optimization_barrier(
        (inverse_rows, c_lo, c_hi, first_lo, first_hi))
    inverse_mine = lax.all_gather(inverse_rows, CHIP_AXES, axis=2, tiled=True)
    conduct_pad = jnp.pad(jnp.concatenate([c_lo, conductivity, c_hi], axis=0), ((0, 0), (1, 1), (1, 1)))
    center_coef, face_coefs = face_terms(conduct_pad)
    y_ids = lax.broadcasted_iota(jnp.int32, center_coef.shape, 1)
    z_ids = lax.broadcasted_iota(jnp.int32, center_coef.shape, 2)
    coefs = [
        center_coef,
        face_coefs[0],
        face_coefs[1],
        jnp.where(y_ids == full_y - 1, 0.0, face_coefs[2]),
        jnp.where(y_ids == 0, 0.0, face_coefs[3]),
        jnp.where(z_ids == depth - 1, 0.0, face_coefs[4]),
        jnp.where(z_ids == 0, 0.0, face_coefs[5]),
    ]
    own_pairs = lax.dynamic_slice_in_dim(electrodes, grp_index * local_src, local_src, 0)
    source_term = source_block(own_pairs, x_start - margin, extended, full_y, full_y, depth)

    mid_planes = list(range(1, width_x - 1))
    bnd_planes = list(range(-margin, 1)) + list(range(width_x - 1, width_x + margin))
    own_planes = list(range(width_x))

    mid_coefs = [c[1 + margin : width_x - 1 + margin] for c in coefs]
    bnd_coefs = [jnp.concatenate([c[: margin + 1], c[width_x - 1 + margin :]], axis=0) for c in coefs]
    own_coefs = [c[margin : margin + width_x] for c in coefs]
    mid_st = source_term[:, 1 + margin : width_x - 1 + margin]
    bnd_st = jnp.concatenate([source_term[:, : margin + 1], source_term[:, width_x - 1 + margin :]], axis=1)
    own_st = source_term[:, margin : margin + width_x]
    mid_coefs, bnd_coefs, own_coefs, mid_st, bnd_st, own_st = lax.optimization_barrier(
        (mid_coefs, bnd_coefs, own_coefs, mid_st, bnd_st, own_st)
    )
    core_vec = jnp.reshape(core, (1,)).astype(jnp.int32)

    columns = []
    for j in range(extended):
        p = j - margin
        if p in mid_planes:
            columns.append((0, mid_planes.index(p)))
        else:
            columns.append((1, bnd_planes.index(p)))

    swap = [(0, 1), (1, 0)]

    potential = potential_init
    for sweep in range(ITERS):
        lo, hi = (first_lo, first_hi) if sweep == 0 else rims_of(potential, rim, 1)
        mid_own, mid_other = stencil_call(mid_planes, core_vec, potential, [], mid_st, mid_coefs, "split")
        mid_got = lax.ppermute(mid_other, CORE, swap)
        bnd_own, bnd_other = stencil_call(bnd_planes, core_vec, potential, [lo, hi], bnd_st, bnd_coefs, "split")
        bnd_got = lax.ppermute(bnd_other, CORE, swap)
        correction = correction_call(
            column_mask, inverse_mine, [mid_own, bnd_own], [mid_got, bnd_got], columns
        ).reshape(2 * local_src, width_x, blocks, rows, depth)
        mine = correction[:local_src]
        back = lax.ppermute(correction[local_src:], CORE, swap)
        first = jnp.where(core == 0, mine, back)
        second = jnp.where(core == 0, back, mine)
        update = jnp.stack([first, second], axis=3).reshape(potential.shape)
        potential = potential + update
    lo, hi = rims_of(potential, 1, 1)
    squares = stencil_call(own_planes, core_vec, potential, [lo, hi], own_st, own_coefs, "norm")
    totals = lax.psum(jnp.sum(squares, axis=(1, 2)), "sub")
    residual_norms = jnp.sqrt(totals / cell_count)
    return (potential, residual_norms)


def solution(mesh):
    n_sub, n_grp = mesh.devices.shape
    n_core = 2
    n_y = 4
    view = Mesh(
        mesh.devices.reshape(n_sub, n_grp // (n_y * n_core), n_y, n_core),
        ("sub", "xl", "y", "core"),
    )
    in_specs = (
        P(GRP, "sub", None, None),
        P("sub", None, None),
        P("sub", None, GRP, None),
        P(),
        P("sub"),
    )
    out_specs = (P(GRP, "sub", None, None), P(GRP))
    return jax.shard_map(
        on_device, mesh=view, in_specs=in_specs, out_specs=out_specs, check_vma=False
    )
```

```python
import jax
import jax.numpy as jnp
from jax import lax
from jax.sharding import Mesh, PartitionSpec as P
from jax.experimental import pallas as pl
from jax.experimental.pallas import tpu as pltpu

ITERS = 2
INTERPRET = False

CURRENT = 16.0
MASS = 1.0

CHIP_AXES = ("xl", "y")
CORE = "core"
GRP = ("xl", "y", "core")


def make_stencil_kernel(planes, has_rim, mode):
    def kernel(core_ref, *refs):
        n_in = 3 if has_rim else 1
        v_ref = refs[0]
        lo_ref, hi_ref = (refs[1], refs[2]) if has_rim else (None, None)
        st_ref, cc_ref, fxp_ref, fxm_ref, fyp_ref, fym_ref, fzp_ref, fzm_ref = refs[n_in : n_in + 8]
        outs = refs[n_in + 8 :]
        width = v_ref.shape[1]
        ny, nz = v_ref.shape[2], v_ref.shape[3]
        core = core_ref[0]

        def load(q):
            if q < 0:
                return lo_ref[0, lo_ref.shape[1] + q]
            if q >= width:
                return hi_ref[0, q - width]
            return v_ref[0, q]

        total = None
        for o, p in enumerate(planes):
            v = load(p)
            image = cc_ref[o] * v
            image = image - fxp_ref[o] * load(p + 1)
            image = image - fxm_ref[o] * load(p - 1)
            image = image - fyp_ref[o] * pltpu.roll(v, ny - 1, 0)
            image = image - fym_ref[o] * pltpu.roll(v, 1, 0)
            image = image - fzp_ref[o] * pltpu.roll(v, nz - 1, 1)
            image = image - fzm_ref[o] * pltpu.roll(v, 1, 1)
            resid = st_ref[0, o] - image
            if mode == "norm":
                square = resid * resid
                total = square if total is None else total + square
                continue
            own_ref, other_ref = outs
            tile = 8
            for g in range(ny // (2 * tile)):
                first = resid[2 * g * tile : (2 * g + 1) * tile]
                second = resid[(2 * g + 1) * tile : (2 * g + 2) * tile]
                own_ref[0, o, g * tile : (g + 1) * tile] = jnp.where(core == 0, first, second)
                other_ref[0, o, g * tile : (g + 1) * tile] = jnp.where(core == 0, second, first)
        if mode == "norm":
            outs[0][0] = total.reshape(ny // 8, 8, nz).sum(axis=0)

    return kernel


def stencil_call(planes, core, v, rims, st, coefs, mode):
    n_src, width, ny, nz = v.shape
    n_out = len(planes)
    own_block = pl.BlockSpec((1, width, ny, nz), lambda s: (s, 0, 0, 0))
    st_block = pl.BlockSpec((1, n_out, ny, nz), lambda s: (s, 0, 0, 0))
    coef_block = pl.BlockSpec((n_out, ny, nz), lambda s: (0, 0, 0))
    rim_specs = [pl.BlockSpec((1, r.shape[1], ny, nz), lambda s: (s, 0, 0, 0)) for r in rims]
    if mode == "norm":
        out_specs = pl.BlockSpec((1, 8, nz), lambda s: (s, 0, 0))
        out_shape = jax.ShapeDtypeStruct((n_src, 8, nz), jnp.float32)
    else:
        half = pl.BlockSpec((1, n_out, ny // 2, nz), lambda s: (s, 0, 0, 0))
        out_specs = [half, half]
        out_shape = [jax.ShapeDtypeStruct((n_src, n_out, ny // 2, nz), jnp.float32)] * 2
    return pl.pallas_call(
        make_stencil_kernel(tuple(planes), len(rims) > 0, mode),
        grid=(n_src,),
        in_specs=[pl.BlockSpec(memory_space=pltpu.SMEM), own_block] + rim_specs + [st_block] + [coef_block] * 7,
        out_specs=out_specs,
        out_shape=out_shape,
        interpret=INTERPRET,
    )(core, v, *rims, st, *coefs)


def make_correction_kernel(columns):
    def kernel(mask_ref, inv_ref, *refs):
        out_ref = refs[-1]
        pieces = refs[:-1]
        n_out = inv_ref.shape[0]
        halves = len(pieces) // 2

        def row(i, carry):
            accs = None
            for j, (piece, plane) in enumerate(columns):
                w = inv_ref[i, j] * mask_ref[j]
                terms = []
                for half in range(2):
                    src_ref = pieces[half * halves + piece]
                    for s in range(src_ref.shape[0]):
                        terms.append(w * src_ref[s, plane])
                accs = terms if accs is None else [a + t for a, t in zip(accs, terms)]
            for s, acc in enumerate(accs):
                out_ref[s, i] = acc
            return carry

        lax.fori_loop(0, n_out, row, 0)

    return kernel


def correction_call(mask, inv, own_pieces, got_pieces, columns, rows=8):
    n_out, n_col, ny, nz = inv.shape
    n_src = sum(p.shape[0] for p in own_pieces[:1]) * 2
    specs = [pl.BlockSpec((p.shape[0], p.shape[1], rows, nz), lambda b: (0, 0, b, 0)) for p in own_pieces + got_pieces]
    return pl.pallas_call(
        make_correction_kernel(tuple(columns)),
        grid=(ny // rows,),
        in_specs=[pl.BlockSpec(memory_space=pltpu.SMEM),
                  pl.BlockSpec((n_out, n_col, rows, nz), lambda b: (0, 0, b, 0))] + specs,
        out_specs=pl.BlockSpec((n_src, n_out, rows, nz), lambda b: (0, 0, b, 0)),
        out_shape=jax.ShapeDtypeStruct((n_src, n_out, ny, nz), jnp.float32),
        interpret=INTERPRET,
    )(mask, inv, *own_pieces, *got_pieces)


def rims_of(cells, depth_x, dim):
    count = lax.axis_size("sub")
    head = lax.slice_in_dim(cells, 0, depth_x, axis=dim)
    tail = lax.slice_in_dim(cells, cells.shape[dim] - depth_x, cells.shape[dim], axis=dim)
    lo = lax.ppermute(tail, "sub", [(i, i + 1) for i in range(count - 1)])
    hi = lax.ppermute(head, "sub", [(i + 1, i) for i in range(count - 1)])
    return lo, hi


def neighbours(padded):
    return [
        padded[..., 2:, 1:-1, 1:-1],
        padded[..., :-2, 1:-1, 1:-1],
        padded[..., 1:-1, 2:, 1:-1],
        padded[..., 1:-1, :-2, 1:-1],
        padded[..., 1:-1, 1:-1, 2:],
        padded[..., 1:-1, 1:-1, :-2],
    ]


def face_terms(conduct_pad):
    center_cells = conduct_pad[1:-1, 1:-1, 1:-1]
    face_coefs = [0.5 * (center_cells + beside_cell) for beside_cell in neighbours(conduct_pad)]
    center_coef = MASS * center_cells
    for face_coef in face_coefs:
        center_coef = center_coef + face_coef
    return (center_coef, face_coefs)


def source_block(pairs, x_start, width_x, rows_y, full_y, depth):
    x_ids = x_start + lax.broadcasted_iota(jnp.int32, (width_x, rows_y, depth), 0)
    y_ids = lax.broadcasted_iota(jnp.int32, (width_x, rows_y, depth), 1)
    z_ids = lax.broadcasted_iota(jnp.int32, (width_x, rows_y, depth), 2)
    flat_ids = (x_ids * full_y + y_ids) * depth + z_ids
    first = (flat_ids[None] == pairs[:, 0][:, None, None, None]).astype(jnp.float32)
    second = (flat_ids[None] == pairs[:, 1][:, None, None, None]).astype(jnp.float32)
    return CURRENT * first - CURRENT * second


def on_device(potential_init, conductivity, inverse_rows, electrodes, intersection_width):
    local_src, width_x, full_y, depth = potential_init.shape
    n_core = lax.axis_size(CORE)
    n_sub = lax.axis_size("sub")
    core = lax.axis_index(CORE)
    grp_index = (lax.axis_index("xl") * lax.axis_size("y") + lax.axis_index("y")) * n_core + core
    sub_index = lax.axis_index("sub")
    extended = inverse_rows.shape[1]
    rows = inverse_rows.shape[2]
    blocks = full_y // (rows * n_core)
    margin = (extended - width_x) // 2
    rim = margin + 1
    cell_count = float(width_x * n_sub * full_y * depth)
    x_start = sub_index * width_x
    column_ids = jnp.arange(extended, dtype=jnp.int32)
    reach = intersection_width[0]
    column_x = x_start - margin + column_ids
    column_mask = (
        (column_ids >= margin - reach)
        & (column_ids < width_x + margin + reach)
        & (column_x >= 0)
        & (column_x < width_x * n_sub)
    ).astype(jnp.float32)
    inverse_mine = lax.all_gather(inverse_rows, CHIP_AXES, axis=2, tiled=True)

    c_lo, c_hi = rims_of(conductivity, rim, 0)
    conduct_pad = jnp.pad(jnp.concatenate([c_lo, conductivity, c_hi], axis=0), ((0, 0), (1, 1), (1, 1)))
    center_coef, face_coefs = face_terms(conduct_pad)
    y_ids = lax.broadcasted_iota(jnp.int32, center_coef.shape, 1)
    z_ids = lax.broadcasted_iota(jnp.int32, center_coef.shape, 2)
    coefs = [
        center_coef,
        face_coefs[0],
        face_coefs[1],
        jnp.where(y_ids == full_y - 1, 0.0, face_coefs[2]),
        jnp.where(y_ids == 0, 0.0, face_coefs[3]),
        jnp.where(z_ids == depth - 1, 0.0, face_coefs[4]),
        jnp.where(z_ids == 0, 0.0, face_coefs[5]),
    ]
    own_pairs = lax.dynamic_slice_in_dim(electrodes, grp_index * local_src, local_src, 0)
    source_term = source_block(own_pairs, x_start - margin, extended, full_y, full_y, depth)

    mid_planes = list(range(1, width_x - 1))
    bnd_planes = list(range(-margin, 1)) + list(range(width_x - 1, width_x + margin))
    own_planes = list(range(width_x))

    mid_coefs = [c[1 + margin : width_x - 1 + margin] for c in coefs]
    bnd_coefs = [jnp.concatenate([c[: margin + 1], c[width_x - 1 + margin :]], axis=0) for c in coefs]
    own_coefs = [c[margin : margin + width_x] for c in coefs]
    mid_st = source_term[:, 1 + margin : width_x - 1 + margin]
    bnd_st = jnp.concatenate([source_term[:, : margin + 1], source_term[:, width_x - 1 + margin :]], axis=1)
    own_st = source_term[:, margin : margin + width_x]
    mid_coefs, bnd_coefs, own_coefs, mid_st, bnd_st, own_st = lax.optimization_barrier(
        (mid_coefs, bnd_coefs, own_coefs, mid_st, bnd_st, own_st)
    )
    core_vec = jnp.reshape(core, (1,)).astype(jnp.int32)

    columns = []
    for j in range(extended):
        p = j - margin
        if p in mid_planes:
            columns.append((0, mid_planes.index(p)))
        else:
            columns.append((1, bnd_planes.index(p)))

    swap = [(0, 1), (1, 0)]

    potential = potential_init
    for sweep in range(ITERS):
        lo, hi = rims_of(potential, rim, 1)
        mid_own, mid_other = stencil_call(mid_planes, core_vec, potential, [], mid_st, mid_coefs, "split")
        mid_got = lax.ppermute(mid_other, CORE, swap)
        bnd_own, bnd_other = stencil_call(bnd_planes, core_vec, potential, [lo, hi], bnd_st, bnd_coefs, "split")
        bnd_got = lax.ppermute(bnd_other, CORE, swap)
        correction = correction_call(
            column_mask, inverse_mine, [mid_own, bnd_own], [mid_got, bnd_got], columns
        ).reshape(2 * local_src, width_x, blocks, rows, depth)
        mine = correction[:local_src]
        back = lax.ppermute(correction[local_src:], CORE, swap)
        first = jnp.where(core == 0, mine, back)
        second = jnp.where(core == 0, back, mine)
        update = jnp.stack([first, second], axis=3).reshape(potential.shape)
        potential = potential + update
    lo, hi = rims_of(potential, 1, 1)
    squares = stencil_call(own_planes, core_vec, potential, [lo, hi], own_st, own_coefs, "norm")
    totals = jnp.sum(squares, axis=(1, 2))
    step_size = 1
    while step_size < n_sub:
        totals = totals + lax.ppermute(totals, "sub", [(i, i ^ step_size) for i in range(n_sub)])
        step_size *= 2
    residual_norms = jnp.sqrt(totals / cell_count)
    return (potential, residual_norms)


def solution(mesh):
    n_sub, n_grp = mesh.devices.shape
    n_core = 2
    n_y = 4
    view = Mesh(
        mesh.devices.reshape(n_sub, n_grp // (n_y * n_core), n_y, n_core),
        ("sub", "xl", "y", "core"),
    )
    in_specs = (
        P(GRP, "sub", None, None),
        P("sub", None, None),
        P("sub", None, GRP, None),
        P(),
        P("sub"),
    )
    out_specs = (P(GRP, "sub", None, None), P(GRP))
    return jax.shard_map(
        on_device, mesh=view, in_specs=in_specs, out_specs=out_specs, check_vma=False
    )
```

```python
import jax
import jax.numpy as jnp
from jax import lax
from jax.sharding import Mesh, PartitionSpec as P
from jax.experimental import pallas as pl
from jax.experimental.pallas import tpu as pltpu

ITERS = 2
INTERPRET = False

CURRENT = 16.0
MASS = 1.0

CHIP_AXES = ("xl", "y")
CORE = "core"
GRP = ("xl", "y", "core")


def make_stencil_kernel(planes, has_rim, mode):
    def kernel(core_ref, *refs):
        n_in = 3 if has_rim else 1
        v_ref = refs[0]
        lo_ref, hi_ref = (refs[1], refs[2]) if has_rim else (None, None)
        st_ref, cc_ref, fxp_ref, fxm_ref, fyp_ref, fym_ref, fzp_ref, fzm_ref = refs[n_in : n_in + 8]
        outs = refs[n_in + 8 :]
        width = v_ref.shape[1]
        ny, nz = v_ref.shape[2], v_ref.shape[3]
        core = core_ref[0]

        def load(q):
            if q < 0:
                return lo_ref[0, lo_ref.shape[1] + q]
            if q >= width:
                return hi_ref[0, q - width]
            return v_ref[0, q]

        total = None
        for o, p in enumerate(planes):
            v = load(p)
            image = cc_ref[o] * v
            image = image - fxp_ref[o] * load(p + 1)
            image = image - fxm_ref[o] * load(p - 1)
            image = image - fyp_ref[o] * pltpu.roll(v, ny - 1, 0)
            image = image - fym_ref[o] * pltpu.roll(v, 1, 0)
            image = image - fzp_ref[o] * pltpu.roll(v, nz - 1, 1)
            image = image - fzm_ref[o] * pltpu.roll(v, 1, 1)
            resid = st_ref[0, o] - image
            if mode == "norm":
                square = resid * resid
                total = square if total is None else total + square
                continue
            own_ref, other_ref = outs
            tile = 8
            for g in range(ny // (2 * tile)):
                first = resid[2 * g * tile : (2 * g + 1) * tile]
                second = resid[(2 * g + 1) * tile : (2 * g + 2) * tile]
                own_ref[0, o, g * tile : (g + 1) * tile] = jnp.where(core == 0, first, second)
                other_ref[0, o, g * tile : (g + 1) * tile] = jnp.where(core == 0, second, first)
        if mode == "norm":
            outs[0][0] = total.reshape(ny // 8, 8, nz).sum(axis=0)

    return kernel


def stencil_call(planes, core, v, rims, st, coefs, mode):
    n_src, width, ny, nz = v.shape
    n_out = len(planes)
    own_block = pl.BlockSpec((1, width, ny, nz), lambda s: (s, 0, 0, 0))
    st_block = pl.BlockSpec((1, n_out, ny, nz), lambda s: (s, 0, 0, 0))
    coef_block = pl.BlockSpec((n_out, ny, nz), lambda s: (0, 0, 0))
    rim_specs = [pl.BlockSpec((1, r.shape[1], ny, nz), lambda s: (s, 0, 0, 0)) for r in rims]
    if mode == "norm":
        out_specs = pl.BlockSpec((1, 8, nz), lambda s: (s, 0, 0))
        out_shape = jax.ShapeDtypeStruct((n_src, 8, nz), jnp.float32)
    else:
        half = pl.BlockSpec((1, n_out, ny // 2, nz), lambda s: (s, 0, 0, 0))
        out_specs = [half, half]
        out_shape = [jax.ShapeDtypeStruct((n_src, n_out, ny // 2, nz), jnp.float32)] * 2
    return pl.pallas_call(
        make_stencil_kernel(tuple(planes), len(rims) > 0, mode),
        grid=(n_src,),
        in_specs=[pl.BlockSpec(memory_space=pltpu.SMEM), own_block] + rim_specs + [st_block] + [coef_block] * 7,
        out_specs=out_specs,
        out_shape=out_shape,
        interpret=INTERPRET,
    )(core, v, *rims, st, *coefs)


def make_correction_kernel(columns, chunk=4):
    def kernel(mask_ref, inv_ref, *refs):
        out_ref = refs[-1]
        pieces = refs[:-1]
        n_out = inv_ref.shape[0]
        halves = len(pieces) // 2

        def rows(c, carry):
            base = c * chunk
            accs = None
            for j, (piece, plane) in enumerate(columns):
                weights = [inv_ref[base + k, j] * mask_ref[j] for k in range(chunk)]
                terms = []
                for half in range(2):
                    src_ref = pieces[half * halves + piece]
                    for s in range(src_ref.shape[0]):
                        value = src_ref[s, plane]
                        terms.append([w * value for w in weights])
                if accs is None:
                    accs = terms
                else:
                    accs = [[a + t for a, t in zip(acc_s, term_s)] for acc_s, term_s in zip(accs, terms)]
            for s, acc_s in enumerate(accs):
                for k in range(chunk):
                    out_ref[s, base + k] = acc_s[k]
            return carry

        lax.fori_loop(0, n_out // chunk, rows, 0)

    return kernel


def correction_call(mask, inv, own_pieces, got_pieces, columns, rows=8):
    n_out, n_col, ny, nz = inv.shape
    n_src = sum(p.shape[0] for p in own_pieces[:1]) * 2
    specs = [pl.BlockSpec((p.shape[0], p.shape[1], rows, nz), lambda b: (0, 0, b, 0)) for p in own_pieces + got_pieces]
    return pl.pallas_call(
        make_correction_kernel(tuple(columns)),
        grid=(ny // rows,),
        in_specs=[pl.BlockSpec(memory_space=pltpu.SMEM),
                  pl.BlockSpec((n_out, n_col, rows, nz), lambda b: (0, 0, b, 0))] + specs,
        out_specs=pl.BlockSpec((n_src, n_out, rows, nz), lambda b: (0, 0, b, 0)),
        out_shape=jax.ShapeDtypeStruct((n_src, n_out, ny, nz), jnp.float32),
        interpret=INTERPRET,
    )(mask, inv, *own_pieces, *got_pieces)


def rims_of(cells, depth_x, dim):
    count = lax.axis_size("sub")
    head = lax.slice_in_dim(cells, 0, depth_x, axis=dim)
    tail = lax.slice_in_dim(cells, cells.shape[dim] - depth_x, cells.shape[dim], axis=dim)
    lo = lax.ppermute(tail, "sub", [(i, i + 1) for i in range(count - 1)])
    hi = lax.ppermute(head, "sub", [(i + 1, i) for i in range(count - 1)])
    return lo, hi


def neighbours(padded):
    return [
        padded[..., 2:, 1:-1, 1:-1],
        padded[..., :-2, 1:-1, 1:-1],
        padded[..., 1:-1, 2:, 1:-1],
        padded[..., 1:-1, :-2, 1:-1],
        padded[..., 1:-1, 1:-1, 2:],
        padded[..., 1:-1, 1:-1, :-2],
    ]


def face_terms(conduct_pad):
    center_cells = conduct_pad[1:-1, 1:-1, 1:-1]
    face_coefs = [0.5 * (center_cells + beside_cell) for beside_cell in neighbours(conduct_pad)]
    center_coef = MASS * center_cells
    for face_coef in face_coefs:
        center_coef = center_coef + face_coef
    return (center_coef, face_coefs)


def source_block(pairs, x_start, width_x, rows_y, full_y, depth):
    x_ids = x_start + lax.broadcasted_iota(jnp.int32, (width_x, rows_y, depth), 0)
    y_ids = lax.broadcasted_iota(jnp.int32, (width_x, rows_y, depth), 1)
    z_ids = lax.broadcasted_iota(jnp.int32, (width_x, rows_y, depth), 2)
    flat_ids = (x_ids * full_y + y_ids) * depth + z_ids
    first = (flat_ids[None] == pairs[:, 0][:, None, None, None]).astype(jnp.float32)
    second = (flat_ids[None] == pairs[:, 1][:, None, None, None]).astype(jnp.float32)
    return CURRENT * first - CURRENT * second


def on_device(potential_init, conductivity, inverse_rows, electrodes, intersection_width):
    local_src, width_x, full_y, depth = potential_init.shape
    n_core = lax.axis_size(CORE)
    n_sub = lax.axis_size("sub")
    core = lax.axis_index(CORE)
    grp_index = (lax.axis_index("xl") * lax.axis_size("y") + lax.axis_index("y")) * n_core + core
    sub_index = lax.axis_index("sub")
    extended = inverse_rows.shape[1]
    rows = inverse_rows.shape[2]
    blocks = full_y // (rows * n_core)
    margin = (extended - width_x) // 2
    rim = margin + 1
    cell_count = float(width_x * n_sub * full_y * depth)
    x_start = sub_index * width_x
    column_ids = jnp.arange(extended, dtype=jnp.int32)
    reach = intersection_width[0]
    column_x = x_start - margin + column_ids
    column_mask = (
        (column_ids >= margin - reach)
        & (column_ids < width_x + margin + reach)
        & (column_x >= 0)
        & (column_x < width_x * n_sub)
    ).astype(jnp.float32)
    inverse_mine = lax.all_gather(inverse_rows, CHIP_AXES, axis=2, tiled=True)

    c_lo, c_hi = rims_of(conductivity, rim, 0)
    conduct_pad = jnp.pad(jnp.concatenate([c_lo, conductivity, c_hi], axis=0), ((0, 0), (1, 1), (1, 1)))
    center_coef, face_coefs = face_terms(conduct_pad)
    y_ids = lax.broadcasted_iota(jnp.int32, center_coef.shape, 1)
    z_ids = lax.broadcasted_iota(jnp.int32, center_coef.shape, 2)
    coefs = [
        center_coef,
        face_coefs[0],
        face_coefs[1],
        jnp.where(y_ids == full_y - 1, 0.0, face_coefs[2]),
        jnp.where(y_ids == 0, 0.0, face_coefs[3]),
        jnp.where(z_ids == depth - 1, 0.0, face_coefs[4]),
        jnp.where(z_ids == 0, 0.0, face_coefs[5]),
    ]
    own_pairs = lax.dynamic_slice_in_dim(electrodes, grp_index * local_src, local_src, 0)
    source_term = source_block(own_pairs, x_start - margin, extended, full_y, full_y, depth)

    mid_planes = list(range(1, width_x - 1))
    bnd_planes = list(range(-margin, 1)) + list(range(width_x - 1, width_x + margin))
    own_planes = list(range(width_x))

    mid_coefs = [c[1 + margin : width_x - 1 + margin] for c in coefs]
    bnd_coefs = [jnp.concatenate([c[: margin + 1], c[width_x - 1 + margin :]], axis=0) for c in coefs]
    own_coefs = [c[margin : margin + width_x] for c in coefs]
    mid_st = source_term[:, 1 + margin : width_x - 1 + margin]
    bnd_st = jnp.concatenate([source_term[:, : margin + 1], source_term[:, width_x - 1 + margin :]], axis=1)
    own_st = source_term[:, margin : margin + width_x]
    mid_coefs, bnd_coefs, own_coefs, mid_st, bnd_st, own_st = lax.optimization_barrier(
        (mid_coefs, bnd_coefs, own_coefs, mid_st, bnd_st, own_st)
    )
    core_vec = jnp.reshape(core, (1,)).astype(jnp.int32)

    columns = []
    for j in range(extended):
        p = j - margin
        if p in mid_planes:
            columns.append((0, mid_planes.index(p)))
        else:
            columns.append((1, bnd_planes.index(p)))

    swap = [(0, 1), (1, 0)]

    potential = potential_init
    for sweep in range(ITERS):
        lo, hi = rims_of(potential, rim, 1)
        mid_own, mid_other = stencil_call(mid_planes, core_vec, potential, [], mid_st, mid_coefs, "split")
        mid_got = lax.ppermute(mid_other, CORE, swap)
        bnd_own, bnd_other = stencil_call(bnd_planes, core_vec, potential, [lo, hi], bnd_st, bnd_coefs, "split")
        bnd_got = lax.ppermute(bnd_other, CORE, swap)
        correction = correction_call(
            column_mask, inverse_mine, [mid_own, bnd_own], [mid_got, bnd_got], columns
        ).reshape(2 * local_src, width_x, blocks, rows, depth)
        mine = correction[:local_src]
        back = lax.ppermute(correction[local_src:], CORE, swap)
        first = jnp.where(core == 0, mine, back)
        second = jnp.where(core == 0, back, mine)
        update = jnp.stack([first, second], axis=3).reshape(potential.shape)
        potential = potential + update
    lo, hi = rims_of(potential, 1, 1)
    squares = stencil_call(own_planes, core_vec, potential, [lo, hi], own_st, own_coefs, "norm")
    totals = jnp.sum(squares, axis=(1, 2))
    step_size = 1
    while step_size < n_sub:
        totals = totals + lax.ppermute(totals, "sub", [(i, i ^ step_size) for i in range(n_sub)])
        step_size *= 2
    residual_norms = jnp.sqrt(totals / cell_count)
    return (potential, residual_norms)


def solution(mesh):
    n_sub, n_grp = mesh.devices.shape
    n_core = 2
    n_y = 4
    view = Mesh(
        mesh.devices.reshape(n_sub, n_grp // (n_y * n_core), n_y, n_core),
        ("sub", "xl", "y", "core"),
    )
    in_specs = (
        P(GRP, "sub", None, None),
        P("sub", None, None),
        P("sub", None, GRP, None),
        P(),
        P("sub"),
    )
    out_specs = (P(GRP, "sub", None, None), P(GRP))
    return jax.shard_map(
        on_device, mesh=view, in_specs=in_specs, out_specs=out_specs, check_vma=False
    )
```

```python
import jax
import jax.numpy as jnp
from jax import lax
from jax.sharding import Mesh, PartitionSpec as P
from jax.experimental import pallas as pl
from jax.experimental.pallas import tpu as pltpu

ITERS = 2
INTERPRET = False

CURRENT = 16.0
MASS = 1.0

CHIP_AXES = ("xl", "y")
CORE = "core"
GRP = ("xl", "y", "core")


def make_stencil_kernel(planes, has_rim, mode):
    def kernel(core_ref, *refs):
        n_in = 3 if has_rim else 1
        v_ref = refs[0]
        lo_ref, hi_ref = (refs[1], refs[2]) if has_rim else (None, None)
        st_ref, cc_ref, fxp_ref, fxm_ref, fyp_ref, fym_ref, fzp_ref, fzm_ref = refs[n_in : n_in + 8]
        outs = refs[n_in + 8 :]
        width = v_ref.shape[1]
        ny, nz = v_ref.shape[2], v_ref.shape[3]
        core = core_ref[0]

        def load(q):
            if q < 0:
                return lo_ref[0, lo_ref.shape[1] + q]
            if q >= width:
                return hi_ref[0, q - width]
            return v_ref[0, q]

        total = None
        for o, p in enumerate(planes):
            v = load(p)
            image = cc_ref[o] * v
            image = image - fxp_ref[o] * load(p + 1)
            image = image - fxm_ref[o] * load(p - 1)
            image = image - fyp_ref[o] * pltpu.roll(v, ny - 1, 0)
            image = image - fym_ref[o] * pltpu.roll(v, 1, 0)
            image = image - fzp_ref[o] * pltpu.roll(v, nz - 1, 1)
            image = image - fzm_ref[o] * pltpu.roll(v, 1, 1)
            resid = st_ref[0, o] - image
            if mode == "norm":
                square = resid * resid
                total = square if total is None else total + square
                continue
            own_ref, other_ref = outs
            tile = 8
            for g in range(ny // (2 * tile)):
                first = resid[2 * g * tile : (2 * g + 1) * tile]
                second = resid[(2 * g + 1) * tile : (2 * g + 2) * tile]
                own_ref[0, o, g * tile : (g + 1) * tile] = jnp.where(core == 0, first, second)
                other_ref[0, o, g * tile : (g + 1) * tile] = jnp.where(core == 0, second, first)
        if mode == "norm":
            outs[0][0] = total.reshape(ny // 8, 8, nz).sum(axis=0)

    return kernel


def stencil_call(planes, core, v, rims, st, coefs, mode):
    n_src, width, ny, nz = v.shape
    n_out = len(planes)
    own_block = pl.BlockSpec((1, width, ny, nz), lambda s: (s, 0, 0, 0))
    st_block = pl.BlockSpec((1, n_out, ny, nz), lambda s: (s, 0, 0, 0))
    coef_block = pl.BlockSpec((n_out, ny, nz), lambda s: (0, 0, 0))
    rim_specs = [pl.BlockSpec((1, r.shape[1], ny, nz), lambda s: (s, 0, 0, 0)) for r in rims]
    if mode == "norm":
        out_specs = pl.BlockSpec((1, 8, nz), lambda s: (s, 0, 0))
        out_shape = jax.ShapeDtypeStruct((n_src, 8, nz), jnp.float32)
    else:
        half = pl.BlockSpec((1, n_out, ny // 2, nz), lambda s: (s, 0, 0, 0))
        out_specs = [half, half]
        out_shape = [jax.ShapeDtypeStruct((n_src, n_out, ny // 2, nz), jnp.float32)] * 2
    return pl.pallas_call(
        make_stencil_kernel(tuple(planes), len(rims) > 0, mode),
        grid=(n_src,),
        in_specs=[pl.BlockSpec(memory_space=pltpu.SMEM), own_block] + rim_specs + [st_block] + [coef_block] * 7,
        out_specs=out_specs,
        out_shape=out_shape,
        interpret=INTERPRET,
    )(core, v, *rims, st, *coefs)


def make_correction_kernel(columns, chunk=2):
    def kernel(mask_ref, inv_ref, *refs):
        out_ref = refs[-1]
        pieces = refs[:-1]
        n_out = inv_ref.shape[0]
        halves = len(pieces) // 2

        def rows(c, carry):
            base = c * chunk
            accs = None
            for j, (piece, plane) in enumerate(columns):
                weights = [inv_ref[base + k, j] * mask_ref[j] for k in range(chunk)]
                terms = []
                for half in range(2):
                    src_ref = pieces[half * halves + piece]
                    for s in range(src_ref.shape[0]):
                        value = src_ref[s, plane]
                        terms.append([w * value for w in weights])
                if accs is None:
                    accs = terms
                else:
                    accs = [[a + t for a, t in zip(acc_s, term_s)] for acc_s, term_s in zip(accs, terms)]
            for s, acc_s in enumerate(accs):
                for k in range(chunk):
                    out_ref[s, base + k] = acc_s[k]
            return carry

        lax.fori_loop(0, n_out // chunk, rows, 0)

    return kernel


def correction_call(mask, inv, own_pieces, got_pieces, columns, rows=16):
    n_out, n_col, ny, nz = inv.shape
    n_src = sum(p.shape[0] for p in own_pieces[:1]) * 2
    specs = [pl.BlockSpec((p.shape[0], p.shape[1], rows, nz), lambda b: (0, 0, b, 0)) for p in own_pieces + got_pieces]
    return pl.pallas_call(
        make_correction_kernel(tuple(columns)),
        grid=(ny // rows,),
        in_specs=[pl.BlockSpec(memory_space=pltpu.SMEM),
                  pl.BlockSpec((n_out, n_col, rows, nz), lambda b: (0, 0, b, 0))] + specs,
        out_specs=pl.BlockSpec((n_src, n_out, rows, nz), lambda b: (0, 0, b, 0)),
        out_shape=jax.ShapeDtypeStruct((n_src, n_out, ny, nz), jnp.float32),
        interpret=INTERPRET,
    )(mask, inv, *own_pieces, *got_pieces)


def rims_of(cells, depth_x, dim):
    count = lax.axis_size("sub")
    head = lax.slice_in_dim(cells, 0, depth_x, axis=dim)
    tail = lax.slice_in_dim(cells, cells.shape[dim] - depth_x, cells.shape[dim], axis=dim)
    lo = lax.ppermute(tail, "sub", [(i, i + 1) for i in range(count - 1)])
    hi = lax.ppermute(head, "sub", [(i + 1, i) for i in range(count - 1)])
    return lo, hi


def neighbours(padded):
    return [
        padded[..., 2:, 1:-1, 1:-1],
        padded[..., :-2, 1:-1, 1:-1],
        padded[..., 1:-1, 2:, 1:-1],
        padded[..., 1:-1, :-2, 1:-1],
        padded[..., 1:-1, 1:-1, 2:],
        padded[..., 1:-1, 1:-1, :-2],
    ]


def face_terms(conduct_pad):
    center_cells = conduct_pad[1:-1, 1:-1, 1:-1]
    face_coefs = [0.5 * (center_cells + beside_cell) for beside_cell in neighbours(conduct_pad)]
    center_coef = MASS * center_cells
    for face_coef in face_coefs:
        center_coef = center_coef + face_coef
    return (center_coef, face_coefs)


def source_block(pairs, x_start, width_x, rows_y, full_y, depth):
    x_ids = x_start + lax.broadcasted_iota(jnp.int32, (width_x, rows_y, depth), 0)
    y_ids = lax.broadcasted_iota(jnp.int32, (width_x, rows_y, depth), 1)
    z_ids = lax.broadcasted_iota(jnp.int32, (width_x, rows_y, depth), 2)
    flat_ids = (x_ids * full_y + y_ids) * depth + z_ids
    first = (flat_ids[None] == pairs[:, 0][:, None, None, None]).astype(jnp.float32)
    second = (flat_ids[None] == pairs[:, 1][:, None, None, None]).astype(jnp.float32)
    return CURRENT * first - CURRENT * second


def on_device(potential_init, conductivity, inverse_rows, electrodes, intersection_width):
    local_src, width_x, full_y, depth = potential_init.shape
    n_core = lax.axis_size(CORE)
    n_sub = lax.axis_size("sub")
    core = lax.axis_index(CORE)
    grp_index = (lax.axis_index("xl") * lax.axis_size("y") + lax.axis_index("y")) * n_core + core
    sub_index = lax.axis_index("sub")
    extended = inverse_rows.shape[1]
    rows = inverse_rows.shape[2]
    blocks = full_y // (rows * n_core)
    margin = (extended - width_x) // 2
    rim = margin + 1
    cell_count = float(width_x * n_sub * full_y * depth)
    x_start = sub_index * width_x
    column_ids = jnp.arange(extended, dtype=jnp.int32)
    reach = intersection_width[0]
    column_x = x_start - margin + column_ids
    column_mask = (
        (column_ids >= margin - reach)
        & (column_ids < width_x + margin + reach)
        & (column_x >= 0)
        & (column_x < width_x * n_sub)
    ).astype(jnp.float32)
    inverse_mine = lax.all_gather(inverse_rows, CHIP_AXES, axis=2, tiled=True)

    c_lo, c_hi = rims_of(conductivity, rim, 0)
    conduct_pad = jnp.pad(jnp.concatenate([c_lo, conductivity, c_hi], axis=0), ((0, 0), (1, 1), (1, 1)))
    center_coef, face_coefs = face_terms(conduct_pad)
    y_ids = lax.broadcasted_iota(jnp.int32, center_coef.shape, 1)
    z_ids = lax.broadcasted_iota(jnp.int32, center_coef.shape, 2)
    coefs = [
        center_coef,
        face_coefs[0],
        face_coefs[1],
        jnp.where(y_ids == full_y - 1, 0.0, face_coefs[2]),
        jnp.where(y_ids == 0, 0.0, face_coefs[3]),
        jnp.where(z_ids == depth - 1, 0.0, face_coefs[4]),
        jnp.where(z_ids == 0, 0.0, face_coefs[5]),
    ]
    own_pairs = lax.dynamic_slice_in_dim(electrodes, grp_index * local_src, local_src, 0)
    source_term = source_block(own_pairs, x_start - margin, extended, full_y, full_y, depth)

    mid_planes = list(range(1, width_x - 1))
    bnd_planes = list(range(-margin, 1)) + list(range(width_x - 1, width_x + margin))
    own_planes = list(range(width_x))

    mid_coefs = [c[1 + margin : width_x - 1 + margin] for c in coefs]
    bnd_coefs = [jnp.concatenate([c[: margin + 1], c[width_x - 1 + margin :]], axis=0) for c in coefs]
    own_coefs = [c[margin : margin + width_x] for c in coefs]
    mid_st = source_term[:, 1 + margin : width_x - 1 + margin]
    bnd_st = jnp.concatenate([source_term[:, : margin + 1], source_term[:, width_x - 1 + margin :]], axis=1)
    own_st = source_term[:, margin : margin + width_x]
    mid_coefs, bnd_coefs, own_coefs, mid_st, bnd_st, own_st = lax.optimization_barrier(
        (mid_coefs, bnd_coefs, own_coefs, mid_st, bnd_st, own_st)
    )
    core_vec = jnp.reshape(core, (1,)).astype(jnp.int32)

    columns = []
    for j in range(extended):
        p = j - margin
        if p in mid_planes:
            columns.append((0, mid_planes.index(p)))
        else:
            columns.append((1, bnd_planes.index(p)))

    swap = [(0, 1), (1, 0)]

    potential = potential_init
    for sweep in range(ITERS):
        lo, hi = rims_of(potential, rim, 1)
        mid_own, mid_other = stencil_call(mid_planes, core_vec, potential, [], mid_st, mid_coefs, "split")
        mid_got = lax.ppermute(mid_other, CORE, swap)
        bnd_own, bnd_other = stencil_call(bnd_planes, core_vec, potential, [lo, hi], bnd_st, bnd_coefs, "split")
        bnd_got = lax.ppermute(bnd_other, CORE, swap)
        correction = correction_call(
            column_mask, inverse_mine, [mid_own, bnd_own], [mid_got, bnd_got], columns
        ).reshape(2 * local_src, width_x, blocks, rows, depth)
        mine = correction[:local_src]
        back = lax.ppermute(correction[local_src:], CORE, swap)
        first = jnp.where(core == 0, mine, back)
        second = jnp.where(core == 0, back, mine)
        update = jnp.stack([first, second], axis=3).reshape(potential.shape)
        potential = potential + update
    lo, hi = rims_of(potential, 1, 1)
    squares = stencil_call(own_planes, core_vec, potential, [lo, hi], own_st, own_coefs, "norm")
    totals = jnp.sum(squares, axis=(1, 2))
    step_size = 1
    while step_size < n_sub:
        totals = totals + lax.ppermute(totals, "sub", [(i, i ^ step_size) for i in range(n_sub)])
        step_size *= 2
    residual_norms = jnp.sqrt(totals / cell_count)
    return (potential, residual_norms)


def solution(mesh):
    n_sub, n_grp = mesh.devices.shape
    n_core = 2
    n_y = 4
    view = Mesh(
        mesh.devices.reshape(n_sub, n_grp // (n_y * n_core), n_y, n_core),
        ("sub", "xl", "y", "core"),
    )
    in_specs = (
        P(GRP, "sub", None, None),
        P("sub", None, None),
        P("sub", None, GRP, None),
        P(),
        P("sub"),
    )
    out_specs = (P(GRP, "sub", None, None), P(GRP))
    return jax.shard_map(
        on_device, mesh=view, in_specs=in_specs, out_specs=out_specs, check_vma=False
    )
```

```python
import jax
import jax.numpy as jnp
from jax import lax
from jax.sharding import Mesh, PartitionSpec as P
from jax.experimental import pallas as pl
from jax.experimental.pallas import tpu as pltpu

ITERS = 2
INTERPRET = False

CURRENT = 16.0
MASS = 1.0

CHIP_AXES = ("xl", "y")
CORE = "core"
GRP = ("xl", "y", "core")


def make_stencil_kernel(planes, has_rim, mode, width, edges):
    def kernel(core_ref, *refs):
        n_v = 2 if edges else 1
        n_in = n_v + (2 if has_rim else 0)
        v_refs = refs[:n_v]
        lo_ref, hi_ref = (refs[n_v], refs[n_v + 1]) if has_rim else (None, None)
        st_ref, cc_ref, fxp_ref, fxm_ref, fyp_ref, fym_ref, fzp_ref, fzm_ref = refs[n_in : n_in + 8]
        outs = refs[n_in + 8 :]
        ny, nz = v_refs[0].shape[2], v_refs[0].shape[3]
        core = core_ref[0]

        def load(q):
            if q < 0:
                return lo_ref[0, lo_ref.shape[1] + q]
            if q >= width:
                return hi_ref[0, q - width]
            if not edges:
                return v_refs[0][0, q]
            if q < EDGE:
                return v_refs[0][0, q]
            return v_refs[1][0, q - (width - EDGE)]

        total = None
        for o, p in enumerate(planes):
            v = load(p)
            image = cc_ref[o] * v
            image = image - fxp_ref[o] * load(p + 1)
            image = image - fxm_ref[o] * load(p - 1)
            image = image - fyp_ref[o] * pltpu.roll(v, ny - 1, 0)
            image = image - fym_ref[o] * pltpu.roll(v, 1, 0)
            image = image - fzp_ref[o] * pltpu.roll(v, nz - 1, 1)
            image = image - fzm_ref[o] * pltpu.roll(v, 1, 1)
            resid = st_ref[0, o] - image
            if mode == "norm":
                square = resid * resid
                total = square if total is None else total + square
                continue
            own_ref, other_ref = outs
            tile = 8
            for g in range(ny // (2 * tile)):
                first = resid[2 * g * tile : (2 * g + 1) * tile]
                second = resid[(2 * g + 1) * tile : (2 * g + 2) * tile]
                own_ref[0, o, g * tile : (g + 1) * tile] = jnp.where(core == 0, first, second)
                other_ref[0, o, g * tile : (g + 1) * tile] = jnp.where(core == 0, second, first)
        if mode == "norm":
            outs[0][0] = total.reshape(ny // 8, 8, nz).sum(axis=0)

    return kernel


EDGE = 2


def stencil_call(planes, core, v, rims, st, coefs, mode):
    n_src, width, ny, nz = v.shape
    n_out = len(planes)
    reads = {q for p in planes for q in (p - 1, p, p + 1) if 0 <= q < width}
    edges = width % EDGE == 0 and width >= 2 * EDGE and all(q < EDGE or q >= width - EDGE for q in reads)
    if edges:
        own_specs = [pl.BlockSpec((1, EDGE, ny, nz), lambda s: (s, 0, 0, 0)),
                     pl.BlockSpec((1, EDGE, ny, nz), lambda s: (s, width // EDGE - 1, 0, 0))]
        own_args = [v, v]
    else:
        own_specs = [pl.BlockSpec((1, width, ny, nz), lambda s: (s, 0, 0, 0))]
        own_args = [v]
    st_block = pl.BlockSpec((1, n_out, ny, nz), lambda s: (s, 0, 0, 0))
    coef_block = pl.BlockSpec((n_out, ny, nz), lambda s: (0, 0, 0))
    rim_specs = [pl.BlockSpec((1, r.shape[1], ny, nz), lambda s: (s, 0, 0, 0)) for r in rims]
    if mode == "norm":
        out_specs = pl.BlockSpec((1, 8, nz), lambda s: (s, 0, 0))
        out_shape = jax.ShapeDtypeStruct((n_src, 8, nz), jnp.float32)
    else:
        half = pl.BlockSpec((1, n_out, ny // 2, nz), lambda s: (s, 0, 0, 0))
        out_specs = [half, half]
        out_shape = [jax.ShapeDtypeStruct((n_src, n_out, ny // 2, nz), jnp.float32)] * 2
    return pl.pallas_call(
        make_stencil_kernel(tuple(planes), len(rims) > 0, mode, width, edges),
        grid=(n_src,),
        in_specs=[pl.BlockSpec(memory_space=pltpu.SMEM)] + own_specs + rim_specs + [st_block] + [coef_block] * 7,
        out_specs=out_specs,
        out_shape=out_shape,
        interpret=INTERPRET,
    )(core, *own_args, *rims, st, *coefs)


def make_correction_kernel(columns, chunk=2):
    def kernel(mask_ref, inv_ref, *refs):
        out_ref = refs[-1]
        pieces = refs[:-1]
        n_out = inv_ref.shape[0]
        halves = len(pieces) // 2

        def rows(c, carry):
            base = c * chunk
            accs = None
            for j, (piece, plane) in enumerate(columns):
                weights = [inv_ref[base + k, j] * mask_ref[j] for k in range(chunk)]
                terms = []
                for half in range(2):
                    src_ref = pieces[half * halves + piece]
                    for s in range(src_ref.shape[0]):
                        value = src_ref[s, plane]
                        terms.append([w * value for w in weights])
                if accs is None:
                    accs = terms
                else:
                    accs = [[a + t for a, t in zip(acc_s, term_s)] for acc_s, term_s in zip(accs, terms)]
            for s, acc_s in enumerate(accs):
                for k in range(chunk):
                    out_ref[s, base + k] = acc_s[k]
            return carry

        lax.fori_loop(0, n_out // chunk, rows, 0)

    return kernel


def correction_call(mask, inv, own_pieces, got_pieces, columns, rows=16):
    n_out, n_col, ny, nz = inv.shape
    n_src = sum(p.shape[0] for p in own_pieces[:1]) * 2
    specs = [pl.BlockSpec((p.shape[0], p.shape[1], rows, nz), lambda b: (0, 0, b, 0)) for p in own_pieces + got_pieces]
    return pl.pallas_call(
        make_correction_kernel(tuple(columns)),
        grid=(ny // rows,),
        in_specs=[pl.BlockSpec(memory_space=pltpu.SMEM),
                  pl.BlockSpec((n_out, n_col, rows, nz), lambda b: (0, 0, b, 0))] + specs,
        out_specs=pl.BlockSpec((n_src, n_out, rows, nz), lambda b: (0, 0, b, 0)),
        out_shape=jax.ShapeDtypeStruct((n_src, n_out, ny, nz), jnp.float32),
        interpret=INTERPRET,
    )(mask, inv, *own_pieces, *got_pieces)


def rims_of(cells, depth_x, dim):
    count = lax.axis_size("sub")
    head = lax.slice_in_dim(cells, 0, depth_x, axis=dim)
    tail = lax.slice_in_dim(cells, cells.shape[dim] - depth_x, cells.shape[dim], axis=dim)
    lo = lax.ppermute(tail, "sub", [(i, i + 1) for i in range(count - 1)])
    hi = lax.ppermute(head, "sub", [(i + 1, i) for i in range(count - 1)])
    return lo, hi


def neighbours(padded):
    return [
        padded[..., 2:, 1:-1, 1:-1],
        padded[..., :-2, 1:-1, 1:-1],
        padded[..., 1:-1, 2:, 1:-1],
        padded[..., 1:-1, :-2, 1:-1],
        padded[..., 1:-1, 1:-1, 2:],
        padded[..., 1:-1, 1:-1, :-2],
    ]


def face_terms(conduct_pad):
    center_cells = conduct_pad[1:-1, 1:-1, 1:-1]
    face_coefs = [0.5 * (center_cells + beside_cell) for beside_cell in neighbours(conduct_pad)]
    center_coef = MASS * center_cells
    for face_coef in face_coefs:
        center_coef = center_coef + face_coef
    return (center_coef, face_coefs)


def source_block(pairs, x_start, width_x, rows_y, full_y, depth):
    x_ids = x_start + lax.broadcasted_iota(jnp.int32, (width_x, rows_y, depth), 0)
    y_ids = lax.broadcasted_iota(jnp.int32, (width_x, rows_y, depth), 1)
    z_ids = lax.broadcasted_iota(jnp.int32, (width_x, rows_y, depth), 2)
    flat_ids = (x_ids * full_y + y_ids) * depth + z_ids
    first = (flat_ids[None] == pairs[:, 0][:, None, None, None]).astype(jnp.float32)
    second = (flat_ids[None] == pairs[:, 1][:, None, None, None]).astype(jnp.float32)
    return CURRENT * first - CURRENT * second


def on_device(potential_init, conductivity, inverse_rows, electrodes, intersection_width):
    local_src, width_x, full_y, depth = potential_init.shape
    n_core = lax.axis_size(CORE)
    n_sub = lax.axis_size("sub")
    core = lax.axis_index(CORE)
    grp_index = (lax.axis_index("xl") * lax.axis_size("y") + lax.axis_index("y")) * n_core + core
    sub_index = lax.axis_index("sub")
    extended = inverse_rows.shape[1]
    rows = inverse_rows.shape[2]
    blocks = full_y // (rows * n_core)
    margin = (extended - width_x) // 2
    rim = margin + 1
    cell_count = float(width_x * n_sub * full_y * depth)
    x_start = sub_index * width_x
    column_ids = jnp.arange(extended, dtype=jnp.int32)
    reach = intersection_width[0]
    column_x = x_start - margin + column_ids
    column_mask = (
        (column_ids >= margin - reach)
        & (column_ids < width_x + margin + reach)
        & (column_x >= 0)
        & (column_x < width_x * n_sub)
    ).astype(jnp.float32)
    inverse_mine = lax.all_gather(inverse_rows, CHIP_AXES, axis=2, tiled=True)

    c_lo, c_hi = rims_of(conductivity, rim, 0)
    conduct_pad = jnp.pad(jnp.concatenate([c_lo, conductivity, c_hi], axis=0), ((0, 0), (1, 1), (1, 1)))
    center_coef, face_coefs = face_terms(conduct_pad)
    y_ids = lax.broadcasted_iota(jnp.int32, center_coef.shape, 1)
    z_ids = lax.broadcasted_iota(jnp.int32, center_coef.shape, 2)
    coefs = [
        center_coef,
        face_coefs[0],
        face_coefs[1],
        jnp.where(y_ids == full_y - 1, 0.0, face_coefs[2]),
        jnp.where(y_ids == 0, 0.0, face_coefs[3]),
        jnp.where(z_ids == depth - 1, 0.0, face_coefs[4]),
        jnp.where(z_ids == 0, 0.0, face_coefs[5]),
    ]
    own_pairs = lax.dynamic_slice_in_dim(electrodes, grp_index * local_src, local_src, 0)
    source_term = source_block(own_pairs, x_start - margin, extended, full_y, full_y, depth)

    mid_planes = list(range(1, width_x - 1))
    bnd_planes = list(range(-margin, 1)) + list(range(width_x - 1, width_x + margin))

    mid_coefs = [c[1 + margin : width_x - 1 + margin] for c in coefs]
    bnd_coefs = [jnp.concatenate([c[: margin + 1], c[width_x - 1 + margin :]], axis=0) for c in coefs]
    edge_planes = [0, width_x - 1]
    edge_coefs = [jnp.concatenate([c[margin : margin + 1], c[margin + width_x - 1 : margin + width_x]], axis=0) for c in coefs]
    edge_st = jnp.concatenate(
        [source_term[:, margin : margin + 1], source_term[:, margin + width_x - 1 : margin + width_x]], axis=1)
    mid_st = source_term[:, 1 + margin : width_x - 1 + margin]
    bnd_st = jnp.concatenate([source_term[:, : margin + 1], source_term[:, width_x - 1 + margin :]], axis=1)
    mid_coefs, bnd_coefs, edge_coefs, mid_st, bnd_st, edge_st = lax.optimization_barrier(
        (mid_coefs, bnd_coefs, edge_coefs, mid_st, bnd_st, edge_st)
    )
    core_vec = jnp.reshape(core, (1,)).astype(jnp.int32)

    columns = []
    for j in range(extended):
        p = j - margin
        if p in mid_planes:
            columns.append((0, mid_planes.index(p)))
        else:
            columns.append((1, bnd_planes.index(p)))

    swap = [(0, 1), (1, 0)]

    potential = potential_init
    for sweep in range(ITERS):
        lo, hi = rims_of(potential, rim, 1)
        mid_own, mid_other = stencil_call(mid_planes, core_vec, potential, [], mid_st, mid_coefs, "split")
        mid_got = lax.ppermute(mid_other, CORE, swap)
        bnd_own, bnd_other = stencil_call(bnd_planes, core_vec, potential, [lo, hi], bnd_st, bnd_coefs, "split")
        bnd_got = lax.ppermute(bnd_other, CORE, swap)
        correction = correction_call(
            column_mask, inverse_mine, [mid_own, bnd_own], [mid_got, bnd_got], columns
        ).reshape(2 * local_src, width_x, blocks, rows, depth)
        mine = correction[:local_src]
        back = lax.ppermute(correction[local_src:], CORE, swap)
        first = jnp.where(core == 0, mine, back)
        second = jnp.where(core == 0, back, mine)
        update = jnp.stack([first, second], axis=3).reshape(potential.shape)
        potential = potential + update
    lo, hi = rims_of(potential, 1, 1)
    inner_squares = stencil_call(mid_planes, core_vec, potential, [], mid_st, mid_coefs, "norm")
    rim_squares = stencil_call(edge_planes, core_vec, potential, [lo, hi], edge_st, edge_coefs, "norm")
    totals = jnp.sum(inner_squares + rim_squares, axis=(1, 2))
    step_size = 1
    while step_size < n_sub:
        totals = totals + lax.ppermute(totals, "sub", [(i, i ^ step_size) for i in range(n_sub)])
        step_size *= 2
    residual_norms = jnp.sqrt(totals / cell_count)
    return (potential, residual_norms)


def solution(mesh):
    n_sub, n_grp = mesh.devices.shape
    n_core = 2
    n_y = 4
    view = Mesh(
        mesh.devices.reshape(n_sub, n_grp // (n_y * n_core), n_y, n_core),
        ("sub", "xl", "y", "core"),
    )
    in_specs = (
        P(GRP, "sub", None, None),
        P("sub", None, None),
        P("sub", None, GRP, None),
        P(),
        P("sub"),
    )
    out_specs = (P(GRP, "sub", None, None), P(GRP))
    return jax.shard_map(
        on_device, mesh=view, in_specs=in_specs, out_specs=out_specs, check_vma=False
    )
```

```python
import jax
import jax.numpy as jnp
from jax import lax
from jax.sharding import Mesh, PartitionSpec as P
from jax.experimental import pallas as pl
from jax.experimental.pallas import tpu as pltpu

ITERS = 2
INTERPRET = False

CURRENT = 16.0
MASS = 1.0

CHIP_AXES = ("xl", "y")
CORE = "core"
GRP = ("xl", "y", "core")


def make_stencil_kernel(planes, has_rim, mode, width, edges):
    def kernel(core_ref, *refs):
        n_v = 2 if edges else 1
        n_in = n_v + (2 if has_rim else 0)
        v_refs = refs[:n_v]
        lo_ref, hi_ref = (refs[n_v], refs[n_v + 1]) if has_rim else (None, None)
        st_ref, cc_ref, fxp_ref, fxm_ref, fyp_ref, fym_ref, fzp_ref, fzm_ref = refs[n_in : n_in + 8]
        outs = refs[n_in + 8 :]
        ny, nz = v_refs[0].shape[2], v_refs[0].shape[3]
        core = core_ref[0]

        def load(q):
            if q < 0:
                return lo_ref[0, lo_ref.shape[1] + q]
            if q >= width:
                return hi_ref[0, q - width]
            if not edges:
                return v_refs[0][0, q]
            if q < EDGE:
                return v_refs[0][0, q]
            return v_refs[1][0, q - (width - EDGE)]

        total = None
        for o, p in enumerate(planes):
            v = load(p)
            image = cc_ref[o] * v
            image = image - fxp_ref[o] * load(p + 1)
            image = image - fxm_ref[o] * load(p - 1)
            image = image - fyp_ref[o] * pltpu.roll(v, ny - 1, 0)
            image = image - fym_ref[o] * pltpu.roll(v, 1, 0)
            image = image - fzp_ref[o] * pltpu.roll(v, nz - 1, 1)
            image = image - fzm_ref[o] * pltpu.roll(v, 1, 1)
            resid = st_ref[0, o] - image
            if mode == "norm":
                square = resid * resid
                total = square if total is None else total + square
                continue
            own_ref, other_ref = outs
            tile = 8
            for g in range(ny // (2 * tile)):
                first = resid[2 * g * tile : (2 * g + 1) * tile]
                second = resid[(2 * g + 1) * tile : (2 * g + 2) * tile]
                own_ref[0, o, g * tile : (g + 1) * tile] = jnp.where(core == 0, first, second)
                other_ref[0, o, g * tile : (g + 1) * tile] = jnp.where(core == 0, second, first)
        if mode == "norm":
            outs[0][0] = total.reshape(ny // 8, 8, nz).sum(axis=0)

    return kernel


EDGE = 2


def stencil_call(planes, core, v, rims, st, coefs, mode):
    n_src, width, ny, nz = v.shape
    n_out = len(planes)
    reads = {q for p in planes for q in (p - 1, p, p + 1) if 0 <= q < width}
    edges = width % EDGE == 0 and width >= 2 * EDGE and all(q < EDGE or q >= width - EDGE for q in reads)
    if edges:
        own_specs = [pl.BlockSpec((1, EDGE, ny, nz), lambda s: (s, 0, 0, 0)),
                     pl.BlockSpec((1, EDGE, ny, nz), lambda s: (s, width // EDGE - 1, 0, 0))]
        own_args = [v, v]
    else:
        own_specs = [pl.BlockSpec((1, width, ny, nz), lambda s: (s, 0, 0, 0))]
        own_args = [v]
    st_block = pl.BlockSpec((1, n_out, ny, nz), lambda s: (s, 0, 0, 0))
    coef_block = pl.BlockSpec((n_out, ny, nz), lambda s: (0, 0, 0))
    rim_specs = [pl.BlockSpec((1, r.shape[1], ny, nz), lambda s: (s, 0, 0, 0)) for r in rims]
    if mode == "norm":
        out_specs = pl.BlockSpec((1, 8, nz), lambda s: (s, 0, 0))
        out_shape = jax.ShapeDtypeStruct((n_src, 8, nz), jnp.float32)
    else:
        half = pl.BlockSpec((1, n_out, ny // 2, nz), lambda s: (s, 0, 0, 0))
        out_specs = [half, half]
        out_shape = [jax.ShapeDtypeStruct((n_src, n_out, ny // 2, nz), jnp.float32)] * 2
    return pl.pallas_call(
        make_stencil_kernel(tuple(planes), len(rims) > 0, mode, width, edges),
        grid=(n_src,),
        in_specs=[pl.BlockSpec(memory_space=pltpu.SMEM)] + own_specs + rim_specs + [st_block] + [coef_block] * 7,
        out_specs=out_specs,
        out_shape=out_shape,
        interpret=INTERPRET,
    )(core, *own_args, *rims, st, *coefs)


def make_correction_kernel(columns, chunk=2):
    def kernel(mask_ref, inv_ref, *refs):
        mine_ref, theirs_ref = refs[-2:]
        pieces = refs[:-2]
        n_out = inv_ref.shape[0]
        halves = len(pieces) // 2

        def rows(c, carry):
            base = c * chunk
            accs = None
            for j, (piece, plane) in enumerate(columns):
                weights = [inv_ref[base + k, j] * mask_ref[j] for k in range(chunk)]
                terms = []
                for half in range(2):
                    src_ref = pieces[half * halves + piece]
                    for s in range(src_ref.shape[0]):
                        value = src_ref[s, plane]
                        terms.append([w * value for w in weights])
                if accs is None:
                    accs = terms
                else:
                    accs = [[a + t for a, t in zip(acc_s, term_s)] for acc_s, term_s in zip(accs, terms)]
            n_half = len(accs) // 2
            for s, acc_s in enumerate(accs):
                dest, slot = (mine_ref, s) if s < n_half else (theirs_ref, s - n_half)
                for k in range(chunk):
                    dest[slot, base + k] = acc_s[k]
            return carry

        lax.fori_loop(0, n_out // chunk, rows, 0)

    return kernel


def correction_call(mask, inv, own_pieces, got_pieces, columns, rows=16):
    n_out, n_col, ny, nz = inv.shape
    n_src = sum(p.shape[0] for p in own_pieces[:1]) * 2
    specs = [pl.BlockSpec((p.shape[0], p.shape[1], rows, nz), lambda b: (0, 0, b, 0)) for p in own_pieces + got_pieces]
    return pl.pallas_call(
        make_correction_kernel(tuple(columns)),
        grid=(ny // rows,),
        in_specs=[pl.BlockSpec(memory_space=pltpu.SMEM),
                  pl.BlockSpec((n_out, n_col, rows, nz), lambda b: (0, 0, b, 0))] + specs,
        out_specs=[pl.BlockSpec((n_src // 2, n_out, rows, nz), lambda b: (0, 0, b, 0))] * 2,
        out_shape=[jax.ShapeDtypeStruct((n_src // 2, n_out, ny, nz), jnp.float32)] * 2,
        interpret=INTERPRET,
    )(mask, inv, *own_pieces, *got_pieces)


def rims_of(cells, depth_x, dim):
    count = lax.axis_size("sub")
    head = lax.slice_in_dim(cells, 0, depth_x, axis=dim)
    tail = lax.slice_in_dim(cells, cells.shape[dim] - depth_x, cells.shape[dim], axis=dim)
    lo = lax.ppermute(tail, "sub", [(i, i + 1) for i in range(count - 1)])
    hi = lax.ppermute(head, "sub", [(i + 1, i) for i in range(count - 1)])
    return lo, hi


def neighbours(padded):
    return [
        padded[..., 2:, 1:-1, 1:-1],
        padded[..., :-2, 1:-1, 1:-1],
        padded[..., 1:-1, 2:, 1:-1],
        padded[..., 1:-1, :-2, 1:-1],
        padded[..., 1:-1, 1:-1, 2:],
        padded[..., 1:-1, 1:-1, :-2],
    ]


def face_terms(conduct_pad):
    center_cells = conduct_pad[1:-1, 1:-1, 1:-1]
    face_coefs = [0.5 * (center_cells + beside_cell) for beside_cell in neighbours(conduct_pad)]
    center_coef = MASS * center_cells
    for face_coef in face_coefs:
        center_coef = center_coef + face_coef
    return (center_coef, face_coefs)


def source_block(pairs, x_start, width_x, rows_y, full_y, depth):
    x_ids = x_start + lax.broadcasted_iota(jnp.int32, (width_x, rows_y, depth), 0)
    y_ids = lax.broadcasted_iota(jnp.int32, (width_x, rows_y, depth), 1)
    z_ids = lax.broadcasted_iota(jnp.int32, (width_x, rows_y, depth), 2)
    flat_ids = (x_ids * full_y + y_ids) * depth + z_ids
    first = (flat_ids[None] == pairs[:, 0][:, None, None, None]).astype(jnp.float32)
    second = (flat_ids[None] == pairs[:, 1][:, None, None, None]).astype(jnp.float32)
    return CURRENT * first - CURRENT * second


def on_device(potential_init, conductivity, inverse_rows, electrodes, intersection_width):
    local_src, width_x, full_y, depth = potential_init.shape
    n_core = lax.axis_size(CORE)
    n_sub = lax.axis_size("sub")
    core = lax.axis_index(CORE)
    grp_index = (lax.axis_index("xl") * lax.axis_size("y") + lax.axis_index("y")) * n_core + core
    sub_index = lax.axis_index("sub")
    extended = inverse_rows.shape[1]
    rows = inverse_rows.shape[2]
    blocks = full_y // (rows * n_core)
    margin = (extended - width_x) // 2
    rim = margin + 1
    cell_count = float(width_x * n_sub * full_y * depth)
    x_start = sub_index * width_x
    column_ids = jnp.arange(extended, dtype=jnp.int32)
    reach = intersection_width[0]
    column_x = x_start - margin + column_ids
    column_mask = (
        (column_ids >= margin - reach)
        & (column_ids < width_x + margin + reach)
        & (column_x >= 0)
        & (column_x < width_x * n_sub)
    ).astype(jnp.float32)
    inverse_mine = lax.all_gather(inverse_rows, CHIP_AXES, axis=2, tiled=True)

    c_lo, c_hi = rims_of(conductivity, rim, 0)
    conduct_pad = jnp.pad(jnp.concatenate([c_lo, conductivity, c_hi], axis=0), ((0, 0), (1, 1), (1, 1)))
    center_coef, face_coefs = face_terms(conduct_pad)
    y_ids = lax.broadcasted_iota(jnp.int32, center_coef.shape, 1)
    z_ids = lax.broadcasted_iota(jnp.int32, center_coef.shape, 2)
    coefs = [
        center_coef,
        face_coefs[0],
        face_coefs[1],
        jnp.where(y_ids == full_y - 1, 0.0, face_coefs[2]),
        jnp.where(y_ids == 0, 0.0, face_coefs[3]),
        jnp.where(z_ids == depth - 1, 0.0, face_coefs[4]),
        jnp.where(z_ids == 0, 0.0, face_coefs[5]),
    ]
    own_pairs = lax.dynamic_slice_in_dim(electrodes, grp_index * local_src, local_src, 0)
    source_term = source_block(own_pairs, x_start - margin, extended, full_y, full_y, depth)

    mid_planes = list(range(1, width_x - 1))
    bnd_planes = list(range(-margin, 1)) + list(range(width_x - 1, width_x + margin))

    mid_coefs = [c[1 + margin : width_x - 1 + margin] for c in coefs]
    bnd_coefs = [jnp.concatenate([c[: margin + 1], c[width_x - 1 + margin :]], axis=0) for c in coefs]
    edge_planes = [0, width_x - 1]
    edge_coefs = [jnp.concatenate([c[margin : margin + 1], c[margin + width_x - 1 : margin + width_x]], axis=0) for c in coefs]
    edge_st = jnp.concatenate(
        [source_term[:, margin : margin + 1], source_term[:, margin + width_x - 1 : margin + width_x]], axis=1)
    mid_st = source_term[:, 1 + margin : width_x - 1 + margin]
    bnd_st = jnp.concatenate([source_term[:, : margin + 1], source_term[:, width_x - 1 + margin :]], axis=1)
    mid_coefs, bnd_coefs, edge_coefs, mid_st, bnd_st, edge_st = lax.optimization_barrier(
        (mid_coefs, bnd_coefs, edge_coefs, mid_st, bnd_st, edge_st)
    )
    core_vec = jnp.reshape(core, (1,)).astype(jnp.int32)

    columns = []
    for j in range(extended):
        p = j - margin
        if p in mid_planes:
            columns.append((0, mid_planes.index(p)))
        else:
            columns.append((1, bnd_planes.index(p)))

    swap = [(0, 1), (1, 0)]

    potential = potential_init
    for sweep in range(ITERS):
        lo, hi = rims_of(potential, rim, 1)
        mid_own, mid_other = stencil_call(mid_planes, core_vec, potential, [], mid_st, mid_coefs, "split")
        mid_got = lax.ppermute(mid_other, CORE, swap)
        bnd_own, bnd_other = stencil_call(bnd_planes, core_vec, potential, [lo, hi], bnd_st, bnd_coefs, "split")
        bnd_got = lax.ppermute(bnd_other, CORE, swap)
        mine, theirs = correction_call(
            column_mask, inverse_mine, [mid_own, bnd_own], [mid_got, bnd_got], columns)
        mine = mine.reshape(local_src, width_x, blocks, rows, depth)
        back = lax.ppermute(theirs, CORE, swap).reshape(local_src, width_x, blocks, rows, depth)
        first = jnp.where(core == 0, mine, back)
        second = jnp.where(core == 0, back, mine)
        update = jnp.stack([first, second], axis=3).reshape(potential.shape)
        potential = potential + update
    lo, hi = rims_of(potential, 1, 1)
    inner_squares = stencil_call(mid_planes, core_vec, potential, [], mid_st, mid_coefs, "norm")
    rim_squares = stencil_call(edge_planes, core_vec, potential, [lo, hi], edge_st, edge_coefs, "norm")
    totals = jnp.sum(inner_squares + rim_squares, axis=(1, 2))
    step_size = 1
    while step_size < n_sub:
        totals = totals + lax.ppermute(totals, "sub", [(i, i ^ step_size) for i in range(n_sub)])
        step_size *= 2
    residual_norms = jnp.sqrt(totals / cell_count)
    return (potential, residual_norms)


def solution(mesh):
    n_sub, n_grp = mesh.devices.shape
    n_core = 2
    n_y = 4
    view = Mesh(
        mesh.devices.reshape(n_sub, n_grp // (n_y * n_core), n_y, n_core),
        ("sub", "xl", "y", "core"),
    )
    in_specs = (
        P(GRP, "sub", None, None),
        P("sub", None, None),
        P("sub", None, GRP, None),
        P(),
        P("sub"),
    )
    out_specs = (P(GRP, "sub", None, None), P(GRP))
    return jax.shard_map(
        on_device, mesh=view, in_specs=in_specs, out_specs=out_specs, check_vma=False
    )
```

```python
import jax
import jax.numpy as jnp
from jax import lax
from jax.sharding import Mesh, PartitionSpec as P
from jax.experimental import pallas as pl
from jax.experimental.pallas import tpu as pltpu

ITERS = 2
INTERPRET = False

CURRENT = 16.0
MASS = 1.0

CHIP_AXES = ("xl", "y")
CORE = "core"
GRP = ("xl", "y", "core")


def make_stencil_kernel(planes, has_rim, mode, width, edges):
    def kernel(core_ref, *refs):
        n_v = 2 if edges else 1
        n_in = n_v + (2 if has_rim else 0)
        v_refs = refs[:n_v]
        lo_ref, hi_ref = (refs[n_v], refs[n_v + 1]) if has_rim else (None, None)
        st_ref, cc_ref, fxp_ref, fxm_ref, fyp_ref, fym_ref, fzp_ref, fzm_ref = refs[n_in : n_in + 8]
        outs = refs[n_in + 8 :]
        ny, nz = v_refs[0].shape[2], v_refs[0].shape[3]
        core = core_ref[0]

        def load(q):
            if q < 0:
                return lo_ref[0, lo_ref.shape[1] + q]
            if q >= width:
                return hi_ref[0, q - width]
            if not edges:
                return v_refs[0][0, q]
            if q < EDGE:
                return v_refs[0][0, q]
            return v_refs[1][0, q - (width - EDGE)]

        total = None
        for o, p in enumerate(planes):
            v = load(p)
            image = cc_ref[o] * v
            image = image - fxp_ref[o] * load(p + 1)
            image = image - fxm_ref[o] * load(p - 1)
            image = image - fyp_ref[o] * pltpu.roll(v, ny - 1, 0)
            image = image - fym_ref[o] * pltpu.roll(v, 1, 0)
            image = image - fzp_ref[o] * pltpu.roll(v, nz - 1, 1)
            image = image - fzm_ref[o] * pltpu.roll(v, 1, 1)
            resid = st_ref[0, o] - image
            if mode == "norm":
                square = resid * resid
                total = square if total is None else total + square
                continue
            own_ref, other_ref = outs
            tile = 8
            for g in range(ny // (2 * tile)):
                first = resid[2 * g * tile : (2 * g + 1) * tile]
                second = resid[(2 * g + 1) * tile : (2 * g + 2) * tile]
                own_ref[0, o, g * tile : (g + 1) * tile] = jnp.where(core == 0, first, second)
                other_ref[0, o, g * tile : (g + 1) * tile] = jnp.where(core == 0, second, first)
        if mode == "norm":
            outs[0][0] = total.reshape(ny // 8, 8, nz).sum(axis=0)

    return kernel


EDGE = 2


def stencil_call(planes, core, v, rims, st, coefs, mode):
    n_src, width, ny, nz = v.shape
    n_out = len(planes)
    reads = {q for p in planes for q in (p - 1, p, p + 1) if 0 <= q < width}
    edges = width % EDGE == 0 and width >= 2 * EDGE and all(q < EDGE or q >= width - EDGE for q in reads)
    if edges:
        own_specs = [pl.BlockSpec((1, EDGE, ny, nz), lambda s: (s, 0, 0, 0)),
                     pl.BlockSpec((1, EDGE, ny, nz), lambda s: (s, width // EDGE - 1, 0, 0))]
        own_args = [v, v]
    else:
        own_specs = [pl.BlockSpec((1, width, ny, nz), lambda s: (s, 0, 0, 0))]
        own_args = [v]
    st_block = pl.BlockSpec((1, n_out, ny, nz), lambda s: (s, 0, 0, 0))
    coef_block = pl.BlockSpec((n_out, ny, nz), lambda s: (0, 0, 0))
    rim_specs = [pl.BlockSpec((1, r.shape[1], ny, nz), lambda s: (s, 0, 0, 0)) for r in rims]
    if mode == "norm":
        out_specs = pl.BlockSpec((1, 8, nz), lambda s: (s, 0, 0))
        out_shape = jax.ShapeDtypeStruct((n_src, 8, nz), jnp.float32)
    else:
        half = pl.BlockSpec((1, n_out, ny // 2, nz), lambda s: (s, 0, 0, 0))
        out_specs = [half, half]
        out_shape = [jax.ShapeDtypeStruct((n_src, n_out, ny // 2, nz), jnp.float32)] * 2
    return pl.pallas_call(
        make_stencil_kernel(tuple(planes), len(rims) > 0, mode, width, edges),
        grid=(n_src,),
        in_specs=[pl.BlockSpec(memory_space=pltpu.SMEM)] + own_specs + rim_specs + [st_block] + [coef_block] * 7,
        out_specs=out_specs,
        out_shape=out_shape,
        interpret=INTERPRET,
    )(core, *own_args, *rims, st, *coefs)


def make_correction_kernel(columns, chunk=1):
    def kernel(mask_ref, inv_ref, *refs):
        mine_ref, theirs_ref = refs[-2:]
        pieces = refs[:-2]
        n_out = inv_ref.shape[0]
        halves = len(pieces) // 2

        def rows(c, carry):
            base = c * chunk
            accs = None
            for j, (piece, plane) in enumerate(columns):
                weights = [inv_ref[base + k, j] * mask_ref[j] for k in range(chunk)]
                terms = []
                for half in range(2):
                    src_ref = pieces[half * halves + piece]
                    for s in range(src_ref.shape[0]):
                        value = src_ref[s, plane]
                        terms.append([w * value for w in weights])
                if accs is None:
                    accs = terms
                else:
                    accs = [[a + t for a, t in zip(acc_s, term_s)] for acc_s, term_s in zip(accs, terms)]
            n_half = len(accs) // 2
            for s, acc_s in enumerate(accs):
                dest, slot = (mine_ref, s) if s < n_half else (theirs_ref, s - n_half)
                for k in range(chunk):
                    dest[slot, base + k] = acc_s[k]
            return carry

        lax.fori_loop(0, n_out // chunk, rows, 0)

    return kernel


def correction_call(mask, inv, own_pieces, got_pieces, columns, rows=32):
    n_out, n_col, ny, nz = inv.shape
    n_src = sum(p.shape[0] for p in own_pieces[:1]) * 2
    specs = [pl.BlockSpec((p.shape[0], p.shape[1], rows, nz), lambda b: (0, 0, b, 0)) for p in own_pieces + got_pieces]
    return pl.pallas_call(
        make_correction_kernel(tuple(columns)),
        grid=(ny // rows,),
        in_specs=[pl.BlockSpec(memory_space=pltpu.SMEM),
                  pl.BlockSpec((n_out, n_col, rows, nz), lambda b: (0, 0, b, 0))] + specs,
        out_specs=[pl.BlockSpec((n_src // 2, n_out, rows, nz), lambda b: (0, 0, b, 0))] * 2,
        out_shape=[jax.ShapeDtypeStruct((n_src // 2, n_out, ny, nz), jnp.float32)] * 2,
        interpret=INTERPRET,
    )(mask, inv, *own_pieces, *got_pieces)


def rims_of(cells, depth_x, dim):
    count = lax.axis_size("sub")
    head = lax.slice_in_dim(cells, 0, depth_x, axis=dim)
    tail = lax.slice_in_dim(cells, cells.shape[dim] - depth_x, cells.shape[dim], axis=dim)
    lo = lax.ppermute(tail, "sub", [(i, i + 1) for i in range(count - 1)])
    hi = lax.ppermute(head, "sub", [(i + 1, i) for i in range(count - 1)])
    return lo, hi


def neighbours(padded):
    return [
        padded[..., 2:, 1:-1, 1:-1],
        padded[..., :-2, 1:-1, 1:-1],
        padded[..., 1:-1, 2:, 1:-1],
        padded[..., 1:-1, :-2, 1:-1],
        padded[..., 1:-1, 1:-1, 2:],
        padded[..., 1:-1, 1:-1, :-2],
    ]


def face_terms(conduct_pad):
    center_cells = conduct_pad[1:-1, 1:-1, 1:-1]
    face_coefs = [0.5 * (center_cells + beside_cell) for beside_cell in neighbours(conduct_pad)]
    center_coef = MASS * center_cells
    for face_coef in face_coefs:
        center_coef = center_coef + face_coef
    return (center_coef, face_coefs)


def source_block(pairs, x_start, width_x, rows_y, full_y, depth):
    x_ids = x_start + lax.broadcasted_iota(jnp.int32, (width_x, rows_y, depth), 0)
    y_ids = lax.broadcasted_iota(jnp.int32, (width_x, rows_y, depth), 1)
    z_ids = lax.broadcasted_iota(jnp.int32, (width_x, rows_y, depth), 2)
    flat_ids = (x_ids * full_y + y_ids) * depth + z_ids
    first = (flat_ids[None] == pairs[:, 0][:, None, None, None]).astype(jnp.float32)
    second = (flat_ids[None] == pairs[:, 1][:, None, None, None]).astype(jnp.float32)
    return CURRENT * first - CURRENT * second


def on_device(potential_init, conductivity, inverse_rows, electrodes, intersection_width):
    local_src, width_x, full_y, depth = potential_init.shape
    n_core = lax.axis_size(CORE)
    n_sub = lax.axis_size("sub")
    core = lax.axis_index(CORE)
    grp_index = (lax.axis_index("xl") * lax.axis_size("y") + lax.axis_index("y")) * n_core + core
    sub_index = lax.axis_index("sub")
    extended = inverse_rows.shape[1]
    rows = inverse_rows.shape[2]
    blocks = full_y // (rows * n_core)
    margin = (extended - width_x) // 2
    rim = margin + 1
    cell_count = float(width_x * n_sub * full_y * depth)
    x_start = sub_index * width_x
    column_ids = jnp.arange(extended, dtype=jnp.int32)
    reach = intersection_width[0]
    column_x = x_start - margin + column_ids
    column_mask = (
        (column_ids >= margin - reach)
        & (column_ids < width_x + margin + reach)
        & (column_x >= 0)
        & (column_x < width_x * n_sub)
    ).astype(jnp.float32)
    inverse_mine = lax.all_gather(inverse_rows, CHIP_AXES, axis=2, tiled=True)

    c_lo, c_hi = rims_of(conductivity, rim, 0)
    conduct_pad = jnp.pad(jnp.concatenate([c_lo, conductivity, c_hi], axis=0), ((0, 0), (1, 1), (1, 1)))
    center_coef, face_coefs = face_terms(conduct_pad)
    y_ids = lax.broadcasted_iota(jnp.int32, center_coef.shape, 1)
    z_ids = lax.broadcasted_iota(jnp.int32, center_coef.shape, 2)
    coefs = [
        center_coef,
        face_coefs[0],
        face_coefs[1],
        jnp.where(y_ids == full_y - 1, 0.0, face_coefs[2]),
        jnp.where(y_ids == 0, 0.0, face_coefs[3]),
        jnp.where(z_ids == depth - 1, 0.0, face_coefs[4]),
        jnp.where(z_ids == 0, 0.0, face_coefs[5]),
    ]
    own_pairs = lax.dynamic_slice_in_dim(electrodes, grp_index * local_src, local_src, 0)
    source_term = source_block(own_pairs, x_start - margin, extended, full_y, full_y, depth)

    mid_planes = list(range(1, width_x - 1))
    bnd_planes = list(range(-margin, 1)) + list(range(width_x - 1, width_x + margin))

    mid_coefs = [c[1 + margin : width_x - 1 + margin] for c in coefs]
    bnd_coefs = [jnp.concatenate([c[: margin + 1], c[width_x - 1 + margin :]], axis=0) for c in coefs]
    edge_planes = [0, width_x - 1]
    edge_coefs = [jnp.concatenate([c[margin : margin + 1], c[margin + width_x - 1 : margin + width_x]], axis=0) for c in coefs]
    edge_st = jnp.concatenate(
        [source_term[:, margin : margin + 1], source_term[:, margin + width_x - 1 : margin + width_x]], axis=1)
    mid_st = source_term[:, 1 + margin : width_x - 1 + margin]
    bnd_st = jnp.concatenate([source_term[:, : margin + 1], source_term[:, width_x - 1 + margin :]], axis=1)
    mid_coefs, bnd_coefs, edge_coefs, mid_st, bnd_st, edge_st = lax.optimization_barrier(
        (mid_coefs, bnd_coefs, edge_coefs, mid_st, bnd_st, edge_st)
    )
    core_vec = jnp.reshape(core, (1,)).astype(jnp.int32)

    columns = []
    for j in range(extended):
        p = j - margin
        if p in mid_planes:
            columns.append((0, mid_planes.index(p)))
        else:
            columns.append((1, bnd_planes.index(p)))

    swap = [(0, 1), (1, 0)]

    potential = potential_init
    for sweep in range(ITERS):
        lo, hi = rims_of(potential, rim, 1)
        mid_own, mid_other = stencil_call(mid_planes, core_vec, potential, [], mid_st, mid_coefs, "split")
        mid_got = lax.ppermute(mid_other, CORE, swap)
        bnd_own, bnd_other = stencil_call(bnd_planes, core_vec, potential, [lo, hi], bnd_st, bnd_coefs, "split")
        bnd_got = lax.ppermute(bnd_other, CORE, swap)
        mine, theirs = correction_call(
            column_mask, inverse_mine, [mid_own, bnd_own], [mid_got, bnd_got], columns)
        mine = mine.reshape(local_src, width_x, blocks, rows, depth)
        back = lax.ppermute(theirs, CORE, swap).reshape(local_src, width_x, blocks, rows, depth)
        first = jnp.where(core == 0, mine, back)
        second = jnp.where(core == 0, back, mine)
        update = jnp.stack([first, second], axis=3).reshape(potential.shape)
        potential = potential + update
    lo, hi = rims_of(potential, 1, 1)
    inner_squares = stencil_call(mid_planes, core_vec, potential, [], mid_st, mid_coefs, "norm")
    rim_squares = stencil_call(edge_planes, core_vec, potential, [lo, hi], edge_st, edge_coefs, "norm")
    totals = jnp.sum(inner_squares + rim_squares, axis=(1, 2))
    step_size = 1
    while step_size < n_sub:
        totals = totals + lax.ppermute(totals, "sub", [(i, i ^ step_size) for i in range(n_sub)])
        step_size *= 2
    residual_norms = jnp.sqrt(totals / cell_count)
    return (potential, residual_norms)


def solution(mesh):
    n_sub, n_grp = mesh.devices.shape
    n_core = 2
    n_y = 4
    view = Mesh(
        mesh.devices.reshape(n_sub, n_grp // (n_y * n_core), n_y, n_core),
        ("sub", "xl", "y", "core"),
    )
    in_specs = (
        P(GRP, "sub", None, None),
        P("sub", None, None),
        P("sub", None, GRP, None),
        P(),
        P("sub"),
    )
    out_specs = (P(GRP, "sub", None, None), P(GRP))
    return jax.shard_map(
        on_device, mesh=view, in_specs=in_specs, out_specs=out_specs, check_vma=False
    )
```
